256 devices in a mesh: cells: 128 (over z, x, y), slab: 2 (over core).
Axes of the slice: x: 4, y: 4, z: 8, core: 2. Of those that a mesh axis runs over, the one named last changes fastest.
Arguments:
- block_owner: int32 [32768], P(('cells', 'slab')), may hold values from 0 to 127, as said below
- contact_elem: int32 [4194304], P(('cells', 'slab')), may hold values from 0 to 8191, as said below
- grain_offset: float32 [3, 4194304], P(None, ('cells', 'slab')), may hold values from -2 to 2
- grain_vel: float32 [3, 4194304], P(None, ('cells', 'slab')), may hold values from -6 to 6
- grain_radius: float32 [4194304], P(('cells', 'slab')), may hold values from 0.5 to 1
- disp_cached: float32 [3, 4194304], P(None, ('cells', 'slab')), may hold values from -1.5 to 1.5
- wall_disp: float32 [3, 128, 16384], P(None, 'slab', 'cells'), may hold values from -4 to 4
- wall_vel: float32 [3, 128, 16384], P(None, 'slab', 'cells'), may hold values from -4 to 4
- wall_stiff: float32 [128, 16384], P('slab', 'cells'), may hold values from 0.5 to 2
Outputs:
- wall_next: float32 [3, 128, 16384], P(None, 'slab', 'cells')
- contact_gap: float32 [4194304], P(('cells', 'slab'))
The draws below stay inside these ranges and needn't reach their ends.
Inputs may be any that keep to these rules, and one draw needn't show every extreme that they name: Tile t of a device is the contacts t * 128 to (t + 1) * 128 - 1 of that device; its contacts touch wall patch block_owner[t] within the device's own height slab. One patch, the outlet, the same for all devices, is named exactly 2 times by every device; every other patch is named at most once by each device (each device's tiles name one patch other than the outlet not at all). The contact touches row contact_elem // 128 and column contact_elem % 128 of its tile's patch.
All inputs are finite; a program needn't handle non-finite values.
Results may differ from the reference program's by a relative error of at most 0.000078.
Values sent between devices are 32-bit elements; how exact they have to be, the bound alone decides.
No kernel may reach another device: no remote copies, remote signals or barrier semaphores. Data moves between devices by JAX's collectives and lax.ppermute only.
A program may use at most 64 MiB of HBM per device.

```python
import math
import jax
import jax.numpy as jnp

ROWS_DEV = 64
COLS_DEV = 128
TILE_ROUNDS = 1
TILE_LEN = 128
SUBSTEPS = 4
PATCHES = 128
HEIGHT_SLABS = 2
TILES_DEV = 128
SOURCES = 256
CONTACTS = 4194304
WALL_ROWS = 128
WALL_COLS = 16384


def contact_plan(key):
    base = jax.random.fold_in(key, 7001)
    outlet = jax.random.randint(jax.random.fold_in(base, 1), (), 0, PATCHES, dtype=jnp.int32)
    dev_keys = jax.random.split(jax.random.fold_in(base, 2), SOURCES)

    def one_device(dev_key):
        first_key, second_key, third_key = jax.random.split(dev_key, 3)
        skipped = (outlet + 1 + jax.random.randint(first_key, (), 0, PATCHES - 1, dtype=jnp.int32)) % PATCHES
        listed = jnp.arange(TILES_DEV, dtype=jnp.int32) // TILE_ROUNDS
        owner = jnp.where(listed == skipped, outlet, listed)
        owner = owner[jax.random.permutation(second_key, TILES_DEV)]
        elements = jax.random.randint(third_key, (TILES_DEV, TILE_LEN), 0, ROWS_DEV * COLS_DEV, dtype=jnp.int32)
        elements = elements.at[0, 0].set(ROWS_DEV * COLS_DEV - 1)
        return (owner, elements.reshape(-1))
    owners, elements = jax.vmap(one_device)(dev_keys)
    return (owners.reshape(-1), elements.reshape(-1))


def draw_block_owner(key, part):
    return contact_plan(key)[0]


def draw_contact_elem(key, part):
    return contact_plan(key)[1]


def block_scale(own_key, extent, cuts, low, top_value):
    def one(position, shards_of):
        heights = jax.random.uniform(jax.random.fold_in(jax.random.fold_in(own_key, 6), position), (shards_of,), jnp.float32, low / len(cuts), top_value / len(cuts))
        return jnp.repeat(jnp.exp(heights), extent[position] // shards_of).reshape((-1,) + (1,) * (len(extent) - position - 1))

    level = one(*cuts[0])
    for cut in cuts[1:]:
        level = level * one(*cut)
    return level


def centred(own_key, extent, scale, bound, cuts=(), kind=jnp.bfloat16):
    loudness = block_scale(own_key, extent, cuts, -0.22, 0.18) if cuts else 1.0
    drawn = jax.random.normal(own_key, extent, jnp.float32) * scale * loudness
    return jnp.minimum(jnp.maximum(drawn, -bound), bound).astype(kind)


def setup_inputs(seed: int = 0) -> dict:
    key_list = jax.random.split(jax.random.key(seed), 10)
    block_owner = draw_block_owner(jax.random.fold_in(key_list[9], 71), 0)
    contact_elem = draw_contact_elem(jax.random.fold_in(key_list[9], 71), 0)
    grain_offset = centred(key_list[2], (3, CONTACTS), 0.3, 2.0, ((1, 256),), jnp.float32)
    grain_vel = centred(key_list[3], (3, CONTACTS), 1.0, 6.0, ((1, 256),), jnp.float32)
    grain_radius = jnp.clip(0.5 + 0.5 * jax.random.uniform(key_list[4], (CONTACTS,), jnp.float32) ** block_scale(key_list[4], (CONTACTS,), ((0, 256),), -0.2, 0.2), 0.5, 1.0)
    disp_cached = centred(key_list[5], (3, CONTACTS), 0.2, 1.5, ((1, 256),), jnp.float32)
    wall_disp = centred(key_list[6], (3, WALL_ROWS, WALL_COLS), 0.5, 4.0, ((1, 2), (2, 128)), jnp.float32)
    wall_vel = centred(key_list[7], (3, WALL_ROWS, WALL_COLS), 0.5, 4.0, ((1, 2), (2, 128)), jnp.float32)
    wall_stiff = jnp.clip(jnp.exp(math.log(2.0) - 1.3862944 * jax.random.uniform(key_list[8], (WALL_ROWS, WALL_COLS), jnp.float32) ** block_scale(key_list[8], (WALL_ROWS, WALL_COLS), ((0, 2), (1, 128)), -0.2, 0.2)), 0.5, 2.0)
    return {"block_owner": block_owner, "contact_elem": contact_elem, "grain_offset": grain_offset, "grain_vel": grain_vel, "grain_radius": grain_radius, "disp_cached": disp_cached, "wall_disp": wall_disp, "wall_vel": wall_vel, "wall_stiff": wall_stiff}


SPRING_RATE = 2.0
SOFTNESS = 0.25
APPROACH_DAMP = 0.5
FRICTION = 0.4
SLIP_SPEED = 0.1
HOOP_RATE = 0.5
SHELL_DAMP = 0.3
TIME_STEP = 0.2
FULL_TURN = 2.0 * math.pi

def normals(column, total_cols):
    angle = (column.astype(jnp.float32) + 0.5) * (FULL_TURN / total_cols)
    return (jnp.cos(angle), jnp.sin(angle))

def contact_push(offset, velocity, radius, cached, facing_cos, facing_sin):
    reach = offset[0] * facing_cos + offset[1] * facing_sin
    intersection = radius + reach - (cached[0] * facing_cos + cached[1] * facing_sin)
    spring = SPRING_RATE * SOFTNESS * jax.nn.softplus(intersection / SOFTNESS)
    approach = velocity[0] * facing_cos + velocity[1] * facing_sin
    pressing = spring + APPROACH_DAMP * approach
    slide_x = velocity[0] - approach * facing_cos
    slide_y = velocity[1] - approach * facing_sin
    slide_z = velocity[2]
    speed = jnp.sqrt(slide_x * slide_x + slide_y * slide_y + slide_z * slide_z + SLIP_SPEED * SLIP_SPEED)
    friction = FRICTION * spring / speed
    push = jnp.stack([pressing * facing_cos + friction * slide_x, pressing * facing_sin + friction * slide_y, friction * slide_z])
    return (push, reach)

def advance(displace, velocity, traction, stiffness, vertical, sideways, facing_cos, facing_sin):
    internal = stiffness * (vertical + sideways - 4.0 * displace)
    radial = HOOP_RATE * stiffness * (displace[0] * facing_cos + displace[1] * facing_sin)
    hoop = jnp.stack([radial * facing_cos, radial * facing_sin, jnp.zeros_like(radial)])
    acceleration = internal - hoop + traction - SHELL_DAMP * velocity
    velocity = velocity + TIME_STEP * acceleration
    return (displace + TIME_STEP * velocity, velocity)

def reference(block_owner, contact_elem, grain_offset, grain_vel, grain_radius, disp_cached, wall_disp, wall_vel, wall_stiff):
    total_cols = COLS_DEV * PATCHES
    total_rows = ROWS_DEV * HEIGHT_SLABS
    counter = jnp.arange(CONTACTS, dtype=jnp.int32)
    source = counter // (TILES_DEV * TILE_LEN)
    patch = block_owner[counter // TILE_LEN]
    row_index = source % HEIGHT_SLABS * ROWS_DEV + contact_elem // COLS_DEV
    col_index = patch * COLS_DEV + contact_elem % COLS_DEV
    facing_cos, facing_sin = normals(col_index, total_cols)
    push, reach = contact_push(grain_offset, grain_vel, grain_radius, disp_cached, facing_cos, facing_sin)
    flat_index = row_index * total_cols + col_index
    traction = jnp.stack([jax.ops.segment_sum(push[component], flat_index, num_segments=total_rows * total_cols) for component in range(3)]).reshape(3, total_rows, total_cols)
    wall_cos, wall_sin = normals(jnp.arange(total_cols, dtype=jnp.int32), total_cols)
    displace, velocity = (wall_disp, wall_vel)
    for substep in range(SUBSTEPS):
        padded = jnp.pad(displace, ((0, 0), (1, 1), (0, 0)))
        vertical = padded[:, 2:] + padded[:, :-2]
        sideways = jnp.roll(displace, -1, axis=2) + jnp.roll(displace, 1, axis=2)
        displace, velocity = advance(displace, velocity, traction, wall_stiff, vertical, sideways, wall_cos, wall_sin)
    landed = displace[0, row_index, col_index] * facing_cos + displace[1, row_index, col_index] * facing_sin
    contact_gap = grain_radius + reach - landed
    return (displace, contact_gap)
```

```python
import math

import jax
import jax.numpy as jnp
from jax import lax
from jax.experimental import pallas as pl
from jax.experimental.pallas import tpu as pltpu
from jax.sharding import PartitionSpec as P

SUBSTEPS = 4


SPRING_RATE = 2.0
SOFTNESS = 0.25
APPROACH_DAMP = 0.5
FRICTION = 0.4
SLIP_SPEED = 0.1
HOOP_RATE = 0.5
SHELL_DAMP = 0.3
TIME_STEP = 0.2
FULL_TURN = 2.0 * math.pi
HIGHEST = lax.Precision.HIGHEST
BF16 = jnp.bfloat16
F32 = jnp.float32


def normals(column, total_cols):
    angle = (column.astype(jnp.float32) + 0.5) * (FULL_TURN / total_cols)
    return (jnp.cos(angle), jnp.sin(angle))


def contact_push(offset, velocity, radius, cached, facing_cos, facing_sin):
    reach = offset[0] * facing_cos + offset[1] * facing_sin
    intersection = radius + reach - (cached[0] * facing_cos + cached[1] * facing_sin)
    spring = SPRING_RATE * SOFTNESS * jax.nn.softplus(intersection / SOFTNESS)
    approach = velocity[0] * facing_cos + velocity[1] * facing_sin
    pressing = spring + APPROACH_DAMP * approach
    slide_x = velocity[0] - approach * facing_cos
    slide_y = velocity[1] - approach * facing_sin
    slide_z = velocity[2]
    speed = jnp.sqrt(
        slide_x * slide_x + slide_y * slide_y + slide_z * slide_z + SLIP_SPEED * SLIP_SPEED
    )
    friction = FRICTION * spring / speed
    push = jnp.stack(
        [
            pressing * facing_cos + friction * slide_x,
            pressing * facing_sin + friction * slide_y,
            friction * slide_z,
        ]
    )
    return (push, reach)


def advance(displace, velocity, traction, stiffness, vertical, sideways, facing_cos, facing_sin):
    internal = stiffness * (vertical + sideways - 4.0 * displace)
    radial = HOOP_RATE * stiffness * (displace[0] * facing_cos + displace[1] * facing_sin)
    hoop = jnp.stack([radial * facing_cos, radial * facing_sin, jnp.zeros_like(radial)])
    acceleration = internal - hoop + traction - SHELL_DAMP * velocity
    velocity = velocity + TIME_STEP * acceleration
    return (displace + TIME_STEP * velocity, velocity)


def to_bf16_grid(x):
    return lax.reduce_precision(x, exponent_bits=8, mantissa_bits=7)


def _split_ids(ids, shift):
    rows = lax.shift_right_logical(ids, jnp.int32(shift))
    cols = jnp.bitwise_and(ids, jnp.int32((1 << shift) - 1))
    return rows, cols


def _scatter_kernel(ids_ref, push_ref, out_ref, *, patch_rows, shift):
    n_rows, lanes = ids_ref.shape
    patch_cols = 1 << shift
    comps = push_ref.shape[0] // 2
    row_iota = lax.broadcasted_iota(jnp.int32, (patch_rows, lanes), 0)
    col_iota = lax.broadcasted_iota(jnp.int32, (patch_cols, lanes), 0)
    out_ref[...] = jnp.zeros_like(out_ref)

    def step(i, carry):
        base = pl.multiple_of(i * 8, 8)
        ids8 = ids_ref[pl.ds(base, 8), :]
        push8 = push_ref[:, pl.ds(base, 8), :]
        total = None
        for g in range(8):
            rows, cols = _split_ids(ids8[g : g + 1, :], shift)
            rhot = (row_iota == rows).astype(BF16)
            chot = (col_iota == cols).astype(BF16)
            his, los = [], []
            for c in range(comps):
                hi = push8[c, g : g + 1, :].astype(BF16)
                lo = push8[comps + c, g : g + 1, :].astype(BF16)
                his.append(rhot * hi)
                los.append(rhot * lo)
            lhs = jnp.concatenate(
                [jnp.concatenate(his, axis=0), jnp.concatenate(los, axis=0)], axis=1
            )
            rhs = jnp.concatenate([chot, chot], axis=1)
            part = lax.dot_general(
                lhs, rhs, (((1,), (1,)), ((), ())), preferred_element_type=F32
            )
            total = part if total is None else total + part
        out_ref[...] += total
        return carry

    lax.fori_loop(0, n_rows // 8, step, 0)


def scatter_traction(ids, push, patch_rows, patch_cols):
    shift = patch_cols.bit_length() - 1
    comps = push.shape[0]
    hi = to_bf16_grid(push)
    parts = jnp.concatenate([hi, push - hi], axis=0)
    kernel = lambda *refs: _scatter_kernel(*refs, patch_rows=patch_rows, shift=shift)
    out = pl.pallas_call(
        kernel,
        out_shape=jax.ShapeDtypeStruct((comps * patch_rows, patch_cols), F32),
        in_specs=[pl.BlockSpec(memory_space=pltpu.VMEM)] * 2,
        out_specs=pl.BlockSpec(memory_space=pltpu.VMEM),
        name="scatter_traction",
    )(ids, parts)
    return out.reshape(comps, patch_rows, patch_cols)


def _gather_kernel(ids_ref, wt_ref, out_ref, *, patch_rows, shift):
    n_rows, lanes = ids_ref.shape
    patch_cols = 1 << shift
    parts = wt_ref.shape[1] // patch_rows
    row_iota = lax.broadcasted_iota(jnp.int32, (patch_rows, lanes), 0)
    col_iota = lax.broadcasted_iota(jnp.int32, (patch_cols, lanes), 0)

    def step(i, carry):
        base = pl.multiple_of(i * 8, 8)
        ids8 = ids_ref[pl.ds(base, 8), :]
        wt = wt_ref[...]
        outs = []
        for g in range(8):
            rows, cols = _split_ids(ids8[g : g + 1, :], shift)
            rhot = (row_iota == rows).astype(BF16)
            rhs = jnp.concatenate([rhot] * parts, axis=0)
            picked = jnp.dot(wt, rhs, preferred_element_type=F32)
            sel = jnp.where(col_iota == cols, picked, 0.0)
            outs.append(jnp.sum(sel, axis=0, keepdims=True))
        out_ref[pl.ds(base, 8), :] = jnp.concatenate(outs, axis=0)
        return carry

    lax.fori_loop(0, n_rows // 8, step, 0)


def gather_field(ids, field):
    patch_rows, patch_cols = field.shape
    shift = patch_cols.bit_length() - 1
    hi = to_bf16_grid(field)
    rest = field - hi
    mid = to_bf16_grid(rest)
    lo = rest - mid
    wt = jnp.concatenate([hi.T, mid.T, lo.T], axis=1).astype(BF16)
    kernel = lambda *refs: _gather_kernel(*refs, patch_rows=patch_rows, shift=shift)
    return pl.pallas_call(
        kernel,
        out_shape=jax.ShapeDtypeStruct(ids.shape, F32),
        in_specs=[pl.BlockSpec(memory_space=pltpu.VMEM)] * 2,
        out_specs=pl.BlockSpec(memory_space=pltpu.VMEM),
        name="gather_field",
    )(ids, wt)


def with_halo(x, width):
    ch, rows, cols = x.shape
    n = lax.axis_size("cells")
    m = lax.axis_size("slab")
    slab = lax.axis_index("slab")
    fwd = [(i, (i + 1) % n) for i in range(n)]
    bwd = [((i + 1) % n, i) for i in range(n)]
    left = lax.ppermute(x[:, :, cols - width :], "cells", fwd)
    right = lax.ppermute(x[:, :, :width], "cells", bwd)
    facing = jnp.where(slab == 0, x[:, rows - width :, :], x[:, :width, :])
    swap = [(j, m - 1 - j) for j in range(m)]
    across = lax.ppermute(facing, "slab", swap)
    diag_fwd = [(i * m + j, ((i + 1) % n) * m + (m - 1 - j)) for i in range(n) for j in range(m)]
    diag_bwd = [(i * m + j, ((i - 1) % n) * m + (m - 1 - j)) for i in range(n) for j in range(m)]
    corner_left = lax.ppermute(facing[:, :, cols - width :], ("cells", "slab"), diag_fwd)
    corner_right = lax.ppermute(facing[:, :, :width], ("cells", "slab"), diag_bwd)
    band = jnp.concatenate([left, x, right], axis=2)
    cap = jnp.concatenate([corner_left, across, corner_right], axis=2)
    zero = jnp.zeros_like(cap)
    top = jnp.where(slab == 0, zero, cap)
    bottom = jnp.where(slab == 0, cap, zero)
    return jnp.concatenate([top, band, bottom], axis=1)


def on_device(
    block_owner,
    contact_elem,
    grain_offset,
    grain_vel,
    grain_radius,
    disp_cached,
    wall_disp,
    wall_vel,
    wall_stiff,
):
    owners = lax.axis_size("cells")
    blocks = block_owner.shape[0]
    tile_len = contact_elem.shape[0] // blocks
    patch_rows, patch_cols = wall_stiff.shape
    total_cols = patch_cols * owners
    capacity = 2 * (blocks // owners)
    slots = owners * capacity
    width = SUBSTEPS
    elements = contact_elem.reshape(blocks, tile_len)
    radius_tiles = grain_radius.reshape(blocks, tile_len)
    col_index = block_owner[:, None] * patch_cols + elements % patch_cols
    facing_cos, facing_sin = normals(col_index, total_cols)
    push, reach = contact_push(
        grain_offset.reshape(3, blocks, tile_len),
        grain_vel.reshape(3, blocks, tile_len),
        radius_tiles,
        disp_cached.reshape(3, blocks, tile_len),
        facing_cos,
        facing_sin,
    )
    patches = jnp.arange(owners, dtype=jnp.int32)
    member = (block_owner[:, None] == patches[None, :]).astype(jnp.float32)
    tile_ids = jnp.arange(blocks, dtype=jnp.int32)
    before = (tile_ids[None, :] < tile_ids[:, None]).astype(jnp.float32)
    earlier = jnp.dot(before, member, precision=HIGHEST)
    slot = block_owner * capacity + jnp.sum(earlier * member, axis=1).astype(jnp.int32)
    placing = (slot[None, :] == jnp.arange(slots, dtype=jnp.int32)[:, None]).astype(jnp.float32)
    payload = jnp.concatenate([push, elements.astype(jnp.float32)[None]], axis=0)
    send = jnp.einsum("sb,cbl->csl", placing, payload, precision=HIGHEST)
    recv = lax.all_to_all(
        send.reshape(4, owners, capacity, tile_len),
        "cells",
        split_axis=1,
        concat_axis=1,
        tiled=True,
    ).reshape(4, slots, tile_len)
    ids_in = recv[3].astype(jnp.int32)

    state = jnp.concatenate([wall_disp, wall_vel, wall_stiff[None]], axis=0)
    state_ext = with_halo(state, width)
    d_ext, v_ext, stiff_ext = state_ext[:3], state_ext[3:6], state_ext[6]

    traction = scatter_traction(ids_in, recv[:3], patch_rows, patch_cols)
    traction_ext = with_halo(traction, width)

    first_col = lax.axis_index("cells") * patch_cols
    ext_cols = (first_col - width + jnp.arange(patch_cols + 2 * width, dtype=jnp.int32)) % total_cols
    ext_cos, ext_sin = normals(ext_cols, total_cols)
    displace, velocity = (d_ext, v_ext)
    for substep in range(SUBSTEPS):
        padded = jnp.pad(displace, ((0, 0), (1, 1), (0, 0)))
        vertical = padded[:, 2:] + padded[:, :-2]
        padded_c = jnp.pad(displace, ((0, 0), (0, 0), (1, 1)))
        sideways = padded_c[:, :, 2:] + padded_c[:, :, :-2]
        displace, velocity = advance(
            displace, velocity, traction_ext, stiff_ext, vertical, sideways, ext_cos, ext_sin
        )
    wall_next = displace[:, width : width + patch_rows, width : width + patch_cols]
    own_cos = ext_cos[width : width + patch_cols]
    own_sin = ext_sin[width : width + patch_cols]
    radial_field = wall_next[0] * own_cos + wall_next[1] * own_sin
    landed_out = gather_field(ids_in, radial_field)
    landed_back = lax.all_to_all(
        landed_out.reshape(owners, capacity, tile_len),
        "cells",
        split_axis=0,
        concat_axis=0,
        tiled=True,
    ).reshape(slots, tile_len)
    landed = jnp.einsum("sb,sl->bl", placing, landed_back, precision=HIGHEST)
    contact_gap = radius_tiles + reach - landed
    return (wall_next, contact_gap.reshape(-1))


def solution(mesh):
    return jax.shard_map(
        on_device,
        mesh=mesh,
        in_specs=(
            P(("cells", "slab")),
            P(("cells", "slab")),
            P(None, ("cells", "slab")),
            P(None, ("cells", "slab")),
            P(("cells", "slab")),
            P(None, ("cells", "slab")),
            P(None, "slab", "cells"),
            P(None, "slab", "cells"),
            P("slab", "cells"),
        ),
        out_specs=(P(None, "slab", "cells"), P(("cells", "slab"))),
        check_vma=False,
    )
```

```python
import math

import jax
import jax.numpy as jnp
from jax import lax
from jax.experimental import pallas as pl
from jax.experimental.pallas import tpu as pltpu
from jax.sharding import PartitionSpec as P

SUBSTEPS = 4


SPRING_RATE = 2.0
SOFTNESS = 0.25
APPROACH_DAMP = 0.5
FRICTION = 0.4
SLIP_SPEED = 0.1
HOOP_RATE = 0.5
SHELL_DAMP = 0.3
TIME_STEP = 0.2
FULL_TURN = 2.0 * math.pi
HIGHEST = lax.Precision.HIGHEST
BF16 = jnp.bfloat16
F32 = jnp.float32


def normals(column, total_cols):
    angle = (column.astype(jnp.float32) + 0.5) * (FULL_TURN / total_cols)
    return (jnp.cos(angle), jnp.sin(angle))


def contact_push(offset, velocity, radius, cached, facing_cos, facing_sin):
    reach = offset[0] * facing_cos + offset[1] * facing_sin
    intersection = radius + reach - (cached[0] * facing_cos + cached[1] * facing_sin)
    spring = SPRING_RATE * SOFTNESS * jax.nn.softplus(intersection / SOFTNESS)
    approach = velocity[0] * facing_cos + velocity[1] * facing_sin
    pressing = spring + APPROACH_DAMP * approach
    slide_x = velocity[0] - approach * facing_cos
    slide_y = velocity[1] - approach * facing_sin
    slide_z = velocity[2]
    speed = jnp.sqrt(
        slide_x * slide_x + slide_y * slide_y + slide_z * slide_z + SLIP_SPEED * SLIP_SPEED
    )
    friction = FRICTION * spring / speed
    push = jnp.stack(
        [
            pressing * facing_cos + friction * slide_x,
            pressing * facing_sin + friction * slide_y,
            friction * slide_z,
        ]
    )
    return (push, reach)


def advance(displace, velocity, traction, stiffness, vertical, sideways, facing_cos, facing_sin):
    internal = stiffness * (vertical + sideways - 4.0 * displace)
    radial = HOOP_RATE * stiffness * (displace[0] * facing_cos + displace[1] * facing_sin)
    hoop = jnp.stack([radial * facing_cos, radial * facing_sin, jnp.zeros_like(radial)])
    acceleration = internal - hoop + traction - SHELL_DAMP * velocity
    velocity = velocity + TIME_STEP * acceleration
    return (displace + TIME_STEP * velocity, velocity)


def to_bf16_grid(x):
    return lax.reduce_precision(x, exponent_bits=8, mantissa_bits=7)


def _split_ids(ids, shift):
    rows = lax.shift_right_logical(ids, jnp.int32(shift))
    cols = jnp.bitwise_and(ids, jnp.int32((1 << shift) - 1))
    return rows, cols


def _scatter_kernel(ids_ref, push_ref, out_ref, *, patch_rows, shift):
    n_rows, lanes = ids_ref.shape
    patch_cols = 1 << shift
    comps = push_ref.shape[0] // 2
    row_iota = lax.broadcasted_iota(jnp.int32, (patch_rows, lanes), 0)
    col_iota = lax.broadcasted_iota(jnp.int32, (patch_cols, lanes), 0)
    out_ref[...] = jnp.zeros_like(out_ref)

    def step(i, carry):
        base = pl.multiple_of(i * 8, 8)
        ids8 = ids_ref[pl.ds(base, 8), :]
        push8 = push_ref[:, pl.ds(base, 8), :]
        total = None
        for g in range(8):
            rows, cols = _split_ids(ids8[g : g + 1, :], shift)
            rhot = (row_iota == rows).astype(BF16)
            chot = (col_iota == cols).astype(BF16)
            his, los = [], []
            for c in range(comps):
                hi = push8[c, g : g + 1, :].astype(BF16)
                lo = push8[comps + c, g : g + 1, :].astype(BF16)
                his.append(rhot * hi)
                los.append(rhot * lo)
            lhs = jnp.concatenate(
                [jnp.concatenate(his, axis=0), jnp.concatenate(los, axis=0)], axis=1
            )
            rhs = jnp.concatenate([chot, chot], axis=1)
            part = lax.dot_general(
                lhs, rhs, (((1,), (1,)), ((), ())), preferred_element_type=F32
            )
            total = part if total is None else total + part
        out_ref[...] += total
        return carry

    lax.fori_loop(0, n_rows // 8, step, 0)


def scatter_traction(ids, push, patch_rows, patch_cols):
    shift = patch_cols.bit_length() - 1
    comps = push.shape[0]
    hi = to_bf16_grid(push)
    parts = jnp.concatenate([hi, push - hi], axis=0)
    kernel = lambda *refs: _scatter_kernel(*refs, patch_rows=patch_rows, shift=shift)
    out = pl.pallas_call(
        kernel,
        out_shape=jax.ShapeDtypeStruct((comps * patch_rows, patch_cols), F32),
        in_specs=[pl.BlockSpec(memory_space=pltpu.VMEM)] * 2,
        out_specs=pl.BlockSpec(memory_space=pltpu.VMEM),
        name="scatter_traction",
    )(ids, parts)
    return out.reshape(comps, patch_rows, patch_cols)


def _gather_kernel(ids_ref, wt_ref, out_ref, *, patch_rows, shift):
    n_rows, lanes = ids_ref.shape
    patch_cols = 1 << shift
    parts = wt_ref.shape[1] // patch_rows
    row_iota = lax.broadcasted_iota(jnp.int32, (patch_rows, lanes), 0)
    col_iota = lax.broadcasted_iota(jnp.int32, (patch_cols, lanes), 0)

    def step(i, carry):
        base = pl.multiple_of(i * 8, 8)
        ids8 = ids_ref[pl.ds(base, 8), :]
        wt = wt_ref[...]
        outs = []
        for g in range(8):
            rows, cols = _split_ids(ids8[g : g + 1, :], shift)
            rhot = (row_iota == rows).astype(BF16)
            rhs = jnp.concatenate([rhot] * parts, axis=0)
            picked = jnp.dot(wt, rhs, preferred_element_type=F32)
            sel = jnp.where(col_iota == cols, picked, 0.0)
            outs.append(jnp.sum(sel, axis=0, keepdims=True))
        out_ref[pl.ds(base, 8), :] = jnp.concatenate(outs, axis=0)
        return carry

    lax.fori_loop(0, n_rows // 8, step, 0)


def gather_field(ids, field):
    patch_rows, patch_cols = field.shape
    shift = patch_cols.bit_length() - 1
    hi = to_bf16_grid(field)
    rest = field - hi
    mid = to_bf16_grid(rest)
    lo = rest - mid
    wt = jnp.concatenate([hi.T, mid.T, lo.T], axis=1).astype(BF16)
    kernel = lambda *refs: _gather_kernel(*refs, patch_rows=patch_rows, shift=shift)
    return pl.pallas_call(
        kernel,
        out_shape=jax.ShapeDtypeStruct(ids.shape, F32),
        in_specs=[pl.BlockSpec(memory_space=pltpu.VMEM)] * 2,
        out_specs=pl.BlockSpec(memory_space=pltpu.VMEM),
        name="gather_field",
    )(ids, wt)


def with_halo(x, width):
    ch, rows, cols = x.shape
    n = lax.axis_size("cells")
    m = lax.axis_size("slab")
    slab = lax.axis_index("slab")
    fwd = [(i, (i + 1) % n) for i in range(n)]
    bwd = [((i + 1) % n, i) for i in range(n)]
    left = lax.ppermute(x[:, :, cols - width :], "cells", fwd)
    right = lax.ppermute(x[:, :, :width], "cells", bwd)
    facing = jnp.where(slab == 0, x[:, rows - width :, :], x[:, :width, :])
    swap = [(j, m - 1 - j) for j in range(m)]
    across = lax.ppermute(facing, "slab", swap)
    diag_fwd = [(i * m + j, ((i + 1) % n) * m + (m - 1 - j)) for i in range(n) for j in range(m)]
    diag_bwd = [(i * m + j, ((i - 1) % n) * m + (m - 1 - j)) for i in range(n) for j in range(m)]
    corner_left = lax.ppermute(facing[:, :, cols - width :], ("cells", "slab"), diag_fwd)
    corner_right = lax.ppermute(facing[:, :, :width], ("cells", "slab"), diag_bwd)
    band = jnp.concatenate([left, x, right], axis=2)
    cap = jnp.concatenate([corner_left, across, corner_right], axis=2)
    zero = jnp.zeros_like(cap)
    top = jnp.where(slab == 0, zero, cap)
    bottom = jnp.where(slab == 0, cap, zero)
    return jnp.concatenate([top, band, bottom], axis=1)


def on_device(
    block_owner,
    contact_elem,
    grain_offset,
    grain_vel,
    grain_radius,
    disp_cached,
    wall_disp,
    wall_vel,
    wall_stiff,
):
    owners = lax.axis_size("cells")
    blocks = block_owner.shape[0]
    tile_len = contact_elem.shape[0] // blocks
    patch_rows, patch_cols = wall_stiff.shape
    total_cols = patch_cols * owners
    capacity = 2 * (blocks // owners)
    slots = owners * capacity
    width = SUBSTEPS
    elements = contact_elem.reshape(blocks, tile_len)
    radius_tiles = grain_radius.reshape(blocks, tile_len)
    col_index = block_owner[:, None] * patch_cols + elements % patch_cols
    facing_cos, facing_sin = normals(col_index, total_cols)
    push, reach = contact_push(
        grain_offset.reshape(3, blocks, tile_len),
        grain_vel.reshape(3, blocks, tile_len),
        radius_tiles,
        disp_cached.reshape(3, blocks, tile_len),
        facing_cos,
        facing_sin,
    )
    patches = jnp.arange(owners, dtype=jnp.int32)
    member = (block_owner[:, None] == patches[None, :]).astype(jnp.float32)
    tile_ids = jnp.arange(blocks, dtype=jnp.int32)
    before = (tile_ids[None, :] < tile_ids[:, None]).astype(jnp.float32)
    earlier = jnp.dot(before, member, precision=HIGHEST)
    slot = block_owner * capacity + jnp.sum(earlier * member, axis=1).astype(jnp.int32)
    placing = (slot[None, :] == jnp.arange(slots, dtype=jnp.int32)[:, None]).astype(jnp.float32)
    payload = jnp.concatenate([push, elements.astype(jnp.float32)[None]], axis=0)
    send = jnp.einsum("sb,cbl->csl", placing, payload, precision=HIGHEST)
    recv = lax.all_to_all(
        send.reshape(4, owners, capacity, tile_len),
        "cells",
        split_axis=1,
        concat_axis=1,
        tiled=True,
    ).reshape(4, slots, tile_len)
    ids_in = recv[3].astype(jnp.int32)

    traction = scatter_traction(ids_in, recv[:3], patch_rows, patch_cols)
    state = jnp.concatenate([wall_disp, wall_vel, wall_stiff[None], traction], axis=0)
    state_ext = with_halo(state, width)
    d_ext, v_ext, stiff_ext = state_ext[:3], state_ext[3:6], state_ext[6]
    traction_ext = state_ext[7:10]

    first_col = lax.axis_index("cells") * patch_cols
    ext_cols = (first_col - width + jnp.arange(patch_cols + 2 * width, dtype=jnp.int32)) % total_cols
    ext_cos, ext_sin = normals(ext_cols, total_cols)
    displace, velocity = (d_ext, v_ext)
    for substep in range(SUBSTEPS):
        padded = jnp.pad(displace, ((0, 0), (1, 1), (0, 0)))
        vertical = padded[:, 2:] + padded[:, :-2]
        padded_c = jnp.pad(displace, ((0, 0), (0, 0), (1, 1)))
        sideways = padded_c[:, :, 2:] + padded_c[:, :, :-2]
        displace, velocity = advance(
            displace, velocity, traction_ext, stiff_ext, vertical, sideways, ext_cos, ext_sin
        )
    wall_next = displace[:, width : width + patch_rows, width : width + patch_cols]
    own_cos = ext_cos[width : width + patch_cols]
    own_sin = ext_sin[width : width + patch_cols]
    radial_field = wall_next[0] * own_cos + wall_next[1] * own_sin
    landed_out = gather_field(ids_in, radial_field)
    landed_back = lax.all_to_all(
        landed_out.reshape(owners, capacity, tile_len),
        "cells",
        split_axis=0,
        concat_axis=0,
        tiled=True,
    ).reshape(slots, tile_len)
    landed = jnp.einsum("sb,sl->bl", placing, landed_back, precision=HIGHEST)
    contact_gap = radius_tiles + reach - landed
    return (wall_next, contact_gap.reshape(-1))


def solution(mesh):
    return jax.shard_map(
        on_device,
        mesh=mesh,
        in_specs=(
            P(("cells", "slab")),
            P(("cells", "slab")),
            P(None, ("cells", "slab")),
            P(None, ("cells", "slab")),
            P(("cells", "slab")),
            P(None, ("cells", "slab")),
            P(None, "slab", "cells"),
            P(None, "slab", "cells"),
            P("slab", "cells"),
        ),
        out_specs=(P(None, "slab", "cells"), P(("cells", "slab"))),
        check_vma=False,
    )
```

```python
import math

import jax
import jax.numpy as jnp
from jax import lax
from jax.experimental import pallas as pl
from jax.experimental.pallas import tpu as pltpu
from jax.sharding import PartitionSpec as P

SUBSTEPS = 4


SPRING_RATE = 2.0
SOFTNESS = 0.25
APPROACH_DAMP = 0.5
FRICTION = 0.4
SLIP_SPEED = 0.1
HOOP_RATE = 0.5
SHELL_DAMP = 0.3
TIME_STEP = 0.2
FULL_TURN = 2.0 * math.pi
HIGHEST = lax.Precision.HIGHEST
BF16 = jnp.bfloat16
F32 = jnp.float32


def normals(column, total_cols):
    angle = (column.astype(jnp.float32) + 0.5) * (FULL_TURN / total_cols)
    return (jnp.cos(angle), jnp.sin(angle))


def contact_push(offset, velocity, radius, cached, facing_cos, facing_sin):
    reach = offset[0] * facing_cos + offset[1] * facing_sin
    intersection = radius + reach - (cached[0] * facing_cos + cached[1] * facing_sin)
    spring = SPRING_RATE * SOFTNESS * jax.nn.softplus(intersection / SOFTNESS)
    approach = velocity[0] * facing_cos + velocity[1] * facing_sin
    pressing = spring + APPROACH_DAMP * approach
    slide_x = velocity[0] - approach * facing_cos
    slide_y = velocity[1] - approach * facing_sin
    slide_z = velocity[2]
    speed = jnp.sqrt(
        slide_x * slide_x + slide_y * slide_y + slide_z * slide_z + SLIP_SPEED * SLIP_SPEED
    )
    friction = FRICTION * spring / speed
    push = jnp.stack(
        [
            pressing * facing_cos + friction * slide_x,
            pressing * facing_sin + friction * slide_y,
            friction * slide_z,
        ]
    )
    return (push, reach)


def advance(displace, velocity, traction, stiffness, vertical, sideways, facing_cos, facing_sin):
    internal = stiffness * (vertical + sideways - 4.0 * displace)
    radial = HOOP_RATE * stiffness * (displace[0] * facing_cos + displace[1] * facing_sin)
    hoop = jnp.stack([radial * facing_cos, radial * facing_sin, jnp.zeros_like(radial)])
    acceleration = internal - hoop + traction - SHELL_DAMP * velocity
    velocity = velocity + TIME_STEP * acceleration
    return (displace + TIME_STEP * velocity, velocity)


def to_bf16_grid(x):
    return lax.reduce_precision(x, exponent_bits=8, mantissa_bits=7)


def _split_ids(ids, shift):
    rows = lax.shift_right_logical(ids, jnp.int32(shift))
    cols = jnp.bitwise_and(ids, jnp.int32((1 << shift) - 1))
    return rows, cols


def _scatter_kernel(count_ref, ids_ref, push_ref, out_ref, *, patch_rows, shift):
    n_rows, lanes = ids_ref.shape
    patch_cols = 1 << shift
    comps = push_ref.shape[0] // 2
    row_iota = lax.broadcasted_iota(jnp.int32, (patch_rows, lanes), 0)
    col_iota = lax.broadcasted_iota(jnp.int32, (patch_cols, lanes), 0)
    out_ref[...] = jnp.zeros_like(out_ref)

    def step(i, carry):
        base = pl.multiple_of(i * 8, 8)
        ids8 = ids_ref[pl.ds(base, 8), :]
        push8 = push_ref[:, pl.ds(base, 8), :]
        total = None
        for g in range(8):
            rows, cols = _split_ids(ids8[g : g + 1, :], shift)
            rhot = (row_iota == rows).astype(BF16)
            chot = (col_iota == cols).astype(BF16)
            his, los = [], []
            for c in range(comps):
                hi = push8[c, g : g + 1, :].astype(BF16)
                lo = push8[comps + c, g : g + 1, :].astype(BF16)
                his.append(rhot * hi)
                los.append(rhot * lo)
            lhs = jnp.concatenate(
                [jnp.concatenate(his, axis=0), jnp.concatenate(los, axis=0)], axis=1
            )
            rhs = jnp.concatenate([chot, chot], axis=1)
            part = lax.dot_general(
                lhs, rhs, (((1,), (1,)), ((), ())), preferred_element_type=F32
            )
            total = part if total is None else total + part
        out_ref[...] += total
        return carry

    lax.fori_loop(0, count_ref[0] // 8, step, 0)


def scatter_traction(count, ids, push, patch_rows, patch_cols):
    shift = patch_cols.bit_length() - 1
    comps = push.shape[0]
    hi = to_bf16_grid(push)
    parts = jnp.concatenate([hi, push - hi], axis=0)
    kernel = lambda *refs: _scatter_kernel(*refs, patch_rows=patch_rows, shift=shift)
    out = pl.pallas_call(
        kernel,
        out_shape=jax.ShapeDtypeStruct((comps * patch_rows, patch_cols), F32),
        in_specs=[pl.BlockSpec(memory_space=pltpu.SMEM)]
        + [pl.BlockSpec(memory_space=pltpu.VMEM)] * 2,
        out_specs=pl.BlockSpec(memory_space=pltpu.VMEM),
        name="scatter_traction",
    )(count, ids, parts)
    return out.reshape(comps, patch_rows, patch_cols)


def _gather_kernel(count_ref, ids_ref, wt_ref, out_ref, *, patch_rows, shift):
    n_rows, lanes = ids_ref.shape
    patch_cols = 1 << shift
    parts = wt_ref.shape[1] // patch_rows
    row_iota = lax.broadcasted_iota(jnp.int32, (patch_rows, lanes), 0)
    col_iota = lax.broadcasted_iota(jnp.int32, (patch_cols, lanes), 0)
    out_ref[...] = jnp.zeros_like(out_ref)

    def step(i, carry):
        base = pl.multiple_of(i * 8, 8)
        ids8 = ids_ref[pl.ds(base, 8), :]
        wt = wt_ref[...]
        outs = []
        for g in range(8):
            rows, cols = _split_ids(ids8[g : g + 1, :], shift)
            rhot = (row_iota == rows).astype(BF16)
            rhs = jnp.concatenate([rhot] * parts, axis=0)
            picked = jnp.dot(wt, rhs, preferred_element_type=F32)
            sel = jnp.where(col_iota == cols, picked, 0.0)
            outs.append(jnp.sum(sel, axis=0, keepdims=True))
        out_ref[pl.ds(base, 8), :] = jnp.concatenate(outs, axis=0)
        return carry

    lax.fori_loop(0, count_ref[0] // 8, step, 0)


def gather_field(count, ids, field):
    patch_rows, patch_cols = field.shape
    shift = patch_cols.bit_length() - 1
    hi = to_bf16_grid(field)
    rest = field - hi
    mid = to_bf16_grid(rest)
    lo = rest - mid
    wt = jnp.concatenate([hi.T, mid.T, lo.T], axis=1).astype(BF16)
    kernel = lambda *refs: _gather_kernel(*refs, patch_rows=patch_rows, shift=shift)
    return pl.pallas_call(
        kernel,
        out_shape=jax.ShapeDtypeStruct(ids.shape, F32),
        in_specs=[pl.BlockSpec(memory_space=pltpu.SMEM)]
        + [pl.BlockSpec(memory_space=pltpu.VMEM)] * 2,
        out_specs=pl.BlockSpec(memory_space=pltpu.VMEM),
        name="gather_field",
    )(count, ids, wt)


def with_halo(x, width):
    ch, rows, cols = x.shape
    n = lax.axis_size("cells")
    m = lax.axis_size("slab")
    slab = lax.axis_index("slab")
    fwd = [(i, (i + 1) % n) for i in range(n)]
    bwd = [((i + 1) % n, i) for i in range(n)]
    left = lax.ppermute(x[:, :, cols - width :], "cells", fwd)
    right = lax.ppermute(x[:, :, :width], "cells", bwd)
    facing = jnp.where(slab == 0, x[:, rows - width :, :], x[:, :width, :])
    swap = [(j, m - 1 - j) for j in range(m)]
    across = lax.ppermute(facing, "slab", swap)
    diag_fwd = [(i * m + j, ((i + 1) % n) * m + (m - 1 - j)) for i in range(n) for j in range(m)]
    diag_bwd = [(i * m + j, ((i - 1) % n) * m + (m - 1 - j)) for i in range(n) for j in range(m)]
    corner_left = lax.ppermute(facing[:, :, cols - width :], ("cells", "slab"), diag_fwd)
    corner_right = lax.ppermute(facing[:, :, :width], ("cells", "slab"), diag_bwd)
    band = jnp.concatenate([left, x, right], axis=2)
    cap = jnp.concatenate([corner_left, across, corner_right], axis=2)
    zero = jnp.zeros_like(cap)
    top = jnp.where(slab == 0, zero, cap)
    bottom = jnp.where(slab == 0, cap, zero)
    return jnp.concatenate([top, band, bottom], axis=1)


def on_device(
    block_owner,
    contact_elem,
    grain_offset,
    grain_vel,
    grain_radius,
    disp_cached,
    wall_disp,
    wall_vel,
    wall_stiff,
):
    owners = lax.axis_size("cells")
    blocks = block_owner.shape[0]
    tile_len = contact_elem.shape[0] // blocks
    patch_rows, patch_cols = wall_stiff.shape
    total_cols = patch_cols * owners
    capacity = 2 * (blocks // owners)
    slots = owners * capacity
    width = SUBSTEPS
    elements = contact_elem.reshape(blocks, tile_len)
    radius_tiles = grain_radius.reshape(blocks, tile_len)
    col_index = block_owner[:, None] * patch_cols + elements % patch_cols
    facing_cos, facing_sin = normals(col_index, total_cols)
    push, reach = contact_push(
        grain_offset.reshape(3, blocks, tile_len),
        grain_vel.reshape(3, blocks, tile_len),
        radius_tiles,
        disp_cached.reshape(3, blocks, tile_len),
        facing_cos,
        facing_sin,
    )
    patches = jnp.arange(owners, dtype=jnp.int32)
    member = (block_owner[:, None] == patches[None, :]).astype(jnp.float32)
    tile_ids = jnp.arange(blocks, dtype=jnp.int32)
    before = (tile_ids[None, :] < tile_ids[:, None]).astype(jnp.float32)
    earlier = jnp.dot(before, member, precision=HIGHEST)
    slot = jnp.sum(earlier * member, axis=1).astype(jnp.int32) * owners + block_owner
    placing = (slot[None, :] == jnp.arange(slots, dtype=jnp.int32)[:, None]).astype(jnp.float32)
    sentinel = patch_rows * patch_cols
    payload = jnp.concatenate([push, elements.astype(jnp.float32)[None]], axis=0)
    send = jnp.einsum("sb,cbl->csl", placing, payload, precision=HIGHEST)
    filled = jnp.sum(placing, axis=1) > 0.5
    send = jnp.concatenate(
        [send[:3], jnp.where(filled[:, None], send[3], float(sentinel))[None]], axis=0
    )
    recv = lax.all_to_all(
        send.reshape(4, capacity, owners, tile_len),
        "cells",
        split_axis=2,
        concat_axis=2,
        tiled=True,
    ).reshape(4, slots, tile_len)
    ids_in = recv[3].astype(jnp.int32)
    round_used = jnp.any(ids_in.reshape(capacity, owners * tile_len) < sentinel, axis=1)
    rounds = jnp.max(jnp.where(round_used, jnp.arange(1, capacity + 1, dtype=jnp.int32), 0))
    count = (rounds * owners).reshape(1)

    traction = scatter_traction(count, ids_in, recv[:3], patch_rows, patch_cols)
    state = jnp.concatenate([wall_disp, wall_vel, wall_stiff[None], traction], axis=0)
    state_ext = with_halo(state, width)
    d_ext, v_ext, stiff_ext = state_ext[:3], state_ext[3:6], state_ext[6]
    traction_ext = state_ext[7:10]

    first_col = lax.axis_index("cells") * patch_cols
    ext_cols = (first_col - width + jnp.arange(patch_cols + 2 * width, dtype=jnp.int32)) % total_cols
    ext_cos, ext_sin = normals(ext_cols, total_cols)
    displace, velocity = (d_ext, v_ext)
    for substep in range(SUBSTEPS):
        padded = jnp.pad(displace, ((0, 0), (1, 1), (0, 0)))
        vertical = padded[:, 2:] + padded[:, :-2]
        padded_c = jnp.pad(displace, ((0, 0), (0, 0), (1, 1)))
        sideways = padded_c[:, :, 2:] + padded_c[:, :, :-2]
        displace, velocity = advance(
            displace, velocity, traction_ext, stiff_ext, vertical, sideways, ext_cos, ext_sin
        )
    wall_next = displace[:, width : width + patch_rows, width : width + patch_cols]
    own_cos = ext_cos[width : width + patch_cols]
    own_sin = ext_sin[width : width + patch_cols]
    radial_field = wall_next[0] * own_cos + wall_next[1] * own_sin
    landed_out = gather_field(count, ids_in, radial_field)
    landed_back = lax.all_to_all(
        landed_out.reshape(capacity, owners, tile_len),
        "cells",
        split_axis=1,
        concat_axis=1,
        tiled=True,
    ).reshape(slots, tile_len)
    landed = jnp.einsum("sb,sl->bl", placing, landed_back, precision=HIGHEST)
    contact_gap = radius_tiles + reach - landed
    return (wall_next, contact_gap.reshape(-1))


def solution(mesh):
    return jax.shard_map(
        on_device,
        mesh=mesh,
        in_specs=(
            P(("cells", "slab")),
            P(("cells", "slab")),
            P(None, ("cells", "slab")),
            P(None, ("cells", "slab")),
            P(("cells", "slab")),
            P(None, ("cells", "slab")),
            P(None, "slab", "cells"),
            P(None, "slab", "cells"),
            P("slab", "cells"),
        ),
        out_specs=(P(None, "slab", "cells"), P(("cells", "slab"))),
        check_vma=False,
    )
```

```python
import math

import jax
import jax.numpy as jnp
from jax import lax
from jax.experimental import pallas as pl
from jax.experimental.pallas import tpu as pltpu
from jax.sharding import PartitionSpec as P

SUBSTEPS = 4


SPRING_RATE = 2.0
SOFTNESS = 0.25
APPROACH_DAMP = 0.5
FRICTION = 0.4
SLIP_SPEED = 0.1
HOOP_RATE = 0.5
SHELL_DAMP = 0.3
TIME_STEP = 0.2
FULL_TURN = 2.0 * math.pi
HIGHEST = lax.Precision.HIGHEST
BF16 = jnp.bfloat16
F32 = jnp.float32


def normals(column, total_cols):
    angle = (column.astype(jnp.float32) + 0.5) * (FULL_TURN / total_cols)
    return (jnp.cos(angle), jnp.sin(angle))


def contact_push(offset, velocity, radius, cached, facing_cos, facing_sin):
    reach = offset[0] * facing_cos + offset[1] * facing_sin
    intersection = radius + reach - (cached[0] * facing_cos + cached[1] * facing_sin)
    spring = SPRING_RATE * SOFTNESS * jax.nn.softplus(intersection / SOFTNESS)
    approach = velocity[0] * facing_cos + velocity[1] * facing_sin
    pressing = spring + APPROACH_DAMP * approach
    slide_x = velocity[0] - approach * facing_cos
    slide_y = velocity[1] - approach * facing_sin
    slide_z = velocity[2]
    speed = jnp.sqrt(
        slide_x * slide_x + slide_y * slide_y + slide_z * slide_z + SLIP_SPEED * SLIP_SPEED
    )
    friction = FRICTION * spring / speed
    push = jnp.stack(
        [
            pressing * facing_cos + friction * slide_x,
            pressing * facing_sin + friction * slide_y,
            friction * slide_z,
        ]
    )
    return (push, reach)


def advance(displace, velocity, traction, stiffness, vertical, sideways, facing_cos, facing_sin):
    internal = stiffness * (vertical + sideways - 4.0 * displace)
    radial = HOOP_RATE * stiffness * (displace[0] * facing_cos + displace[1] * facing_sin)
    hoop = jnp.stack([radial * facing_cos, radial * facing_sin, jnp.zeros_like(radial)])
    acceleration = internal - hoop + traction - SHELL_DAMP * velocity
    velocity = velocity + TIME_STEP * acceleration
    return (displace + TIME_STEP * velocity, velocity)


def to_bf16_grid(x):
    return lax.reduce_precision(x, exponent_bits=8, mantissa_bits=7)


def _split_ids(ids, shift):
    rows = lax.shift_right_logical(ids, jnp.int32(shift))
    cols = jnp.bitwise_and(ids, jnp.int32((1 << shift) - 1))
    return rows, cols


def _scatter_kernel(count_ref, recv_ref, out_ref, *, patch_rows, shift):
    comps = recv_ref.shape[0] - 1
    lanes = recv_ref.shape[2]
    patch_cols = 1 << shift
    row_iota = lax.broadcasted_iota(jnp.int32, (patch_rows, lanes), 0)
    col_iota = lax.broadcasted_iota(jnp.int32, (patch_cols, lanes), 0)
    out_ref[...] = jnp.zeros_like(out_ref)

    def step(i, carry):
        base = pl.multiple_of(i * 8, 8)
        blk = recv_ref[:, pl.ds(base, 8), :]
        ids8 = blk[comps].astype(jnp.int32)
        total = None
        for g in range(8):
            rows, cols = _split_ids(ids8[g : g + 1, :], shift)
            rhot = (row_iota == rows).astype(BF16)
            chot = (col_iota == cols).astype(BF16)
            his, los = [], []
            for c in range(comps):
                p = blk[c, g : g + 1, :]
                hi = p.astype(BF16)
                lo = (p - hi.astype(F32)).astype(BF16)
                his.append(rhot * hi)
                los.append(rhot * lo)
            lhs = jnp.concatenate(
                [jnp.concatenate(his, axis=0), jnp.concatenate(los, axis=0)], axis=1
            )
            rhs = jnp.concatenate([chot, chot], axis=1)
            part = lax.dot_general(
                lhs, rhs, (((1,), (1,)), ((), ())), preferred_element_type=F32
            )
            total = part if total is None else total + part
        out_ref[...] += total
        return carry

    lax.fori_loop(0, count_ref[0] // 8, step, 0)


def scatter_traction(count, recv, patch_rows, patch_cols):
    shift = patch_cols.bit_length() - 1
    comps = recv.shape[0] - 1
    kernel = lambda *refs: _scatter_kernel(*refs, patch_rows=patch_rows, shift=shift)
    out = pl.pallas_call(
        kernel,
        out_shape=jax.ShapeDtypeStruct((comps * patch_rows, patch_cols), F32),
        in_specs=[pl.BlockSpec(memory_space=pltpu.SMEM), pl.BlockSpec(memory_space=pltpu.VMEM)],
        out_specs=pl.BlockSpec(memory_space=pltpu.VMEM),
        name="scatter_traction",
    )(count, recv)
    return out.reshape(comps, patch_rows, patch_cols)


def _gather_kernel(count_ref, recv_ref, wt_ref, out_ref, *, patch_rows, shift):
    owners = out_ref.shape[0]
    lanes = recv_ref.shape[2]
    id_row = recv_ref.shape[0] - 1
    patch_cols = 1 << shift
    parts = wt_ref.shape[1] // patch_rows
    row_iota = lax.broadcasted_iota(jnp.int32, (patch_rows, lanes), 0)
    col_iota = lax.broadcasted_iota(jnp.int32, (patch_cols, lanes), 0)
    out_ref[...] = jnp.zeros_like(out_ref)

    def step(i, carry):
        base = pl.multiple_of(i * 8, 8)
        ids8 = recv_ref[id_row, pl.ds(base, 8), :].astype(jnp.int32)
        wt = wt_ref[...]
        outs = []
        for g in range(8):
            rows, cols = _split_ids(ids8[g : g + 1, :], shift)
            rhot = (row_iota == rows).astype(BF16)
            rhs = jnp.concatenate([rhot] * parts, axis=0)
            picked = jnp.dot(wt, rhs, preferred_element_type=F32)
            sel = jnp.where(col_iota == cols, picked, 0.0)
            outs.append(jnp.sum(sel, axis=0, keepdims=True))
        rnd = base // owners
        first = pl.multiple_of(base - rnd * owners, 8)
        out_ref[pl.ds(first, 8), rnd, :] = jnp.concatenate(outs, axis=0)
        return carry

    lax.fori_loop(0, count_ref[0] // 8, step, 0)


def gather_field(count, recv, field, owners, capacity):
    patch_rows, patch_cols = field.shape
    shift = patch_cols.bit_length() - 1
    hi = to_bf16_grid(field)
    rest = field - hi
    mid = to_bf16_grid(rest)
    lo = rest - mid
    wt = jnp.concatenate([hi.T, mid.T, lo.T], axis=1).astype(BF16)
    kernel = lambda *refs: _gather_kernel(*refs, patch_rows=patch_rows, shift=shift)
    return pl.pallas_call(
        kernel,
        out_shape=jax.ShapeDtypeStruct((owners, capacity, recv.shape[2]), F32),
        in_specs=[pl.BlockSpec(memory_space=pltpu.SMEM)]
        + [pl.BlockSpec(memory_space=pltpu.VMEM)] * 2,
        out_specs=pl.BlockSpec(memory_space=pltpu.VMEM),
        name="gather_field",
    )(count, recv, wt)


def with_halo(x, width):
    ch, rows, cols = x.shape
    n = lax.axis_size("cells")
    m = lax.axis_size("slab")
    slab = lax.axis_index("slab")
    fwd = [(i, (i + 1) % n) for i in range(n)]
    bwd = [((i + 1) % n, i) for i in range(n)]
    left = lax.ppermute(x[:, :, cols - width :], "cells", fwd)
    right = lax.ppermute(x[:, :, :width], "cells", bwd)
    facing = jnp.where(slab == 0, x[:, rows - width :, :], x[:, :width, :])
    swap = [(j, m - 1 - j) for j in range(m)]
    across = lax.ppermute(facing, "slab", swap)
    diag_fwd = [(i * m + j, ((i + 1) % n) * m + (m - 1 - j)) for i in range(n) for j in range(m)]
    diag_bwd = [(i * m + j, ((i - 1) % n) * m + (m - 1 - j)) for i in range(n) for j in range(m)]
    corner_left = lax.ppermute(facing[:, :, cols - width :], ("cells", "slab"), diag_fwd)
    corner_right = lax.ppermute(facing[:, :, :width], ("cells", "slab"), diag_bwd)
    band = jnp.concatenate([left, x, right], axis=2)
    cap = jnp.concatenate([corner_left, across, corner_right], axis=2)
    zero = jnp.zeros_like(cap)
    top = jnp.where(slab == 0, zero, cap)
    bottom = jnp.where(slab == 0, cap, zero)
    return jnp.concatenate([top, band, bottom], axis=1)


def on_device(
    block_owner,
    contact_elem,
    grain_offset,
    grain_vel,
    grain_radius,
    disp_cached,
    wall_disp,
    wall_vel,
    wall_stiff,
):
    owners = lax.axis_size("cells")
    blocks = block_owner.shape[0]
    tile_len = contact_elem.shape[0] // blocks
    patch_rows, patch_cols = wall_stiff.shape
    total_cols = patch_cols * owners
    capacity = 2 * (blocks // owners)
    slots = owners * capacity
    width = SUBSTEPS
    elements = contact_elem.reshape(blocks, tile_len)
    radius_tiles = grain_radius.reshape(blocks, tile_len)
    col_index = block_owner[:, None] * patch_cols + elements % patch_cols
    facing_cos, facing_sin = normals(col_index, total_cols)
    push, reach = contact_push(
        grain_offset.reshape(3, blocks, tile_len),
        grain_vel.reshape(3, blocks, tile_len),
        radius_tiles,
        disp_cached.reshape(3, blocks, tile_len),
        facing_cos,
        facing_sin,
    )
    patches = jnp.arange(owners, dtype=jnp.int32)
    member = (block_owner[:, None] == patches[None, :]).astype(jnp.float32)
    tile_ids = jnp.arange(blocks, dtype=jnp.int32)
    before = (tile_ids[None, :] < tile_ids[:, None]).astype(jnp.float32)
    earlier = jnp.dot(before, member, precision=HIGHEST)
    slot = jnp.sum(earlier * member, axis=1).astype(jnp.int32) * owners + block_owner
    placing = (slot[None, :] == jnp.arange(slots, dtype=jnp.int32)[:, None]).astype(jnp.float32)
    sentinel = patch_rows * patch_cols
    payload = jnp.concatenate([push, elements.astype(jnp.float32)[None]], axis=0)
    send = jnp.einsum("sb,cbl->csl", placing, payload, precision=HIGHEST)
    filled = jnp.sum(placing, axis=1) > 0.5
    send = jnp.concatenate(
        [send[:3], jnp.where(filled[:, None], send[3], float(sentinel))[None]], axis=0
    )
    recv = lax.all_to_all(
        send.reshape(4, capacity, owners, tile_len),
        "cells",
        split_axis=2,
        concat_axis=2,
        tiled=True,
    ).reshape(4, slots, tile_len)
    round_used = jnp.any(recv[3].reshape(capacity, owners * tile_len) < sentinel, axis=1)
    rounds = jnp.max(jnp.where(round_used, jnp.arange(1, capacity + 1, dtype=jnp.int32), 0))
    count = (rounds * owners).reshape(1)

    traction = scatter_traction(count, recv, patch_rows, patch_cols)
    state = jnp.concatenate([wall_disp, wall_vel, wall_stiff[None], traction], axis=0)
    state_ext = with_halo(state, width)
    d_ext, v_ext, stiff_ext = state_ext[:3], state_ext[3:6], state_ext[6]
    traction_ext = state_ext[7:10]

    first_col = lax.axis_index("cells") * patch_cols
    ext_cols = (first_col - width + jnp.arange(patch_cols + 2 * width, dtype=jnp.int32)) % total_cols
    ext_cos, ext_sin = normals(ext_cols, total_cols)
    displace, velocity = (d_ext, v_ext)
    for substep in range(SUBSTEPS):
        padded = jnp.pad(displace, ((0, 0), (1, 1), (0, 0)))
        vertical = padded[:, 2:] + padded[:, :-2]
        padded_c = jnp.pad(displace, ((0, 0), (0, 0), (1, 1)))
        sideways = padded_c[:, :, 2:] + padded_c[:, :, :-2]
        displace, velocity = advance(
            displace, velocity, traction_ext, stiff_ext, vertical, sideways, ext_cos, ext_sin
        )
    wall_next = displace[:, width : width + patch_rows, width : width + patch_cols]
    own_cos = ext_cos[width : width + patch_cols]
    own_sin = ext_sin[width : width + patch_cols]
    radial_field = wall_next[0] * own_cos + wall_next[1] * own_sin
    landed_out = gather_field(count, recv, radial_field, owners, capacity)
    landed_back = lax.all_to_all(
        landed_out, "cells", split_axis=0, concat_axis=0, tiled=True
    ).reshape(slots, tile_len)
    back_slot = block_owner * capacity + jnp.sum(earlier * member, axis=1).astype(jnp.int32)
    taking = (back_slot[None, :] == jnp.arange(slots, dtype=jnp.int32)[:, None]).astype(jnp.float32)
    landed = jnp.einsum("sb,sl->bl", taking, landed_back, precision=HIGHEST)
    contact_gap = radius_tiles + reach - landed
    return (wall_next, contact_gap.reshape(-1))


def solution(mesh):
    return jax.shard_map(
        on_device,
        mesh=mesh,
        in_specs=(
            P(("cells", "slab")),
            P(("cells", "slab")),
            P(None, ("cells", "slab")),
            P(None, ("cells", "slab")),
            P(("cells", "slab")),
            P(None, ("cells", "slab")),
            P(None, "slab", "cells"),
            P(None, "slab", "cells"),
            P("slab", "cells"),
        ),
        out_specs=(P(None, "slab", "cells"), P(("cells", "slab"))),
        check_vma=False,
    )
```

```python
import math

import jax
import jax.numpy as jnp
from jax import lax
from jax.experimental import pallas as pl
from jax.experimental.pallas import tpu as pltpu
from jax.sharding import PartitionSpec as P

SUBSTEPS = 4


SPRING_RATE = 2.0
SOFTNESS = 0.25
APPROACH_DAMP = 0.5
FRICTION = 0.4
SLIP_SPEED = 0.1
HOOP_RATE = 0.5
SHELL_DAMP = 0.3
TIME_STEP = 0.2
FULL_TURN = 2.0 * math.pi
HIGHEST = lax.Precision.HIGHEST
BF16 = jnp.bfloat16
F32 = jnp.float32


def normals(column, total_cols):
    angle = (column.astype(jnp.float32) + 0.5) * (FULL_TURN / total_cols)
    return (jnp.cos(angle), jnp.sin(angle))


def contact_push(offset, velocity, radius, cached, facing_cos, facing_sin):
    reach = offset[0] * facing_cos + offset[1] * facing_sin
    intersection = radius + reach - (cached[0] * facing_cos + cached[1] * facing_sin)
    spring = SPRING_RATE * SOFTNESS * jax.nn.softplus(intersection / SOFTNESS)
    approach = velocity[0] * facing_cos + velocity[1] * facing_sin
    pressing = spring + APPROACH_DAMP * approach
    slide_x = velocity[0] - approach * facing_cos
    slide_y = velocity[1] - approach * facing_sin
    slide_z = velocity[2]
    speed = jnp.sqrt(
        slide_x * slide_x + slide_y * slide_y + slide_z * slide_z + SLIP_SPEED * SLIP_SPEED
    )
    friction = FRICTION * spring / speed
    push = jnp.stack(
        [
            pressing * facing_cos + friction * slide_x,
            pressing * facing_sin + friction * slide_y,
            friction * slide_z,
        ]
    )
    return (push, reach)


def advance(displace, velocity, traction, stiffness, vertical, sideways, facing_cos, facing_sin):
    internal = stiffness * (vertical + sideways - 4.0 * displace)
    radial = HOOP_RATE * stiffness * (displace[0] * facing_cos + displace[1] * facing_sin)
    hoop = jnp.stack([radial * facing_cos, radial * facing_sin, jnp.zeros_like(radial)])
    acceleration = internal - hoop + traction - SHELL_DAMP * velocity
    velocity = velocity + TIME_STEP * acceleration
    return (displace + TIME_STEP * velocity, velocity)


def to_bf16_grid(x):
    return lax.reduce_precision(x, exponent_bits=8, mantissa_bits=7)


def _split_ids(ids, shift):
    rows = lax.shift_right_logical(ids, jnp.int32(shift))
    cols = jnp.bitwise_and(ids, jnp.int32((1 << shift) - 1))
    return rows, cols


def _scatter_kernel(count_ref, recv_ref, out_ref, *, patch_rows, shift):
    comps = recv_ref.shape[0] - 1
    lanes = recv_ref.shape[2]
    patch_cols = 1 << shift
    row_iota = lax.broadcasted_iota(jnp.int32, (patch_rows, lanes), 0)
    col_iota = lax.broadcasted_iota(jnp.int32, (patch_cols, lanes), 0)
    out_ref[...] = jnp.zeros_like(out_ref)

    def step(i, carry):
        base = pl.multiple_of(i * 8, 8)
        blk = recv_ref[:, pl.ds(base, 8), :]
        ids8 = blk[comps].astype(jnp.int32)
        total = None
        for g in range(8):
            rows, cols = _split_ids(ids8[g : g + 1, :], shift)
            rhot = (row_iota == rows).astype(BF16)
            chot = (col_iota == cols).astype(BF16)
            his, los = [], []
            for c in range(comps):
                p = blk[c, g : g + 1, :]
                hi = p.astype(BF16)
                lo = (p - hi.astype(F32)).astype(BF16)
                his.append(rhot * hi)
                los.append(rhot * lo)
            lhs = jnp.concatenate(
                [jnp.concatenate(his, axis=0), jnp.concatenate(los, axis=0)], axis=1
            )
            rhs = jnp.concatenate([chot, chot], axis=1)
            part = lax.dot_general(
                lhs, rhs, (((1,), (1,)), ((), ())), preferred_element_type=F32
            )
            total = part if total is None else total + part
        out_ref[...] += total
        return carry

    lax.fori_loop(0, count_ref[0] // 8, step, 0)


def scatter_traction(count, recv, patch_rows, patch_cols):
    shift = patch_cols.bit_length() - 1
    comps = recv.shape[0] - 1
    kernel = lambda *refs: _scatter_kernel(*refs, patch_rows=patch_rows, shift=shift)
    out = pl.pallas_call(
        kernel,
        out_shape=jax.ShapeDtypeStruct((comps * patch_rows, patch_cols), F32),
        in_specs=[pl.BlockSpec(memory_space=pltpu.SMEM), pl.BlockSpec(memory_space=pltpu.VMEM)],
        out_specs=pl.BlockSpec(memory_space=pltpu.VMEM),
        name="scatter_traction",
    )(count, recv)
    return out.reshape(comps, patch_rows, patch_cols)


def _gather_kernel(count_ref, recv_ref, wt_ref, out_ref, *, patch_rows, shift):
    owners = out_ref.shape[0]
    lanes = recv_ref.shape[2]
    id_row = recv_ref.shape[0] - 1
    patch_cols = 1 << shift
    parts = wt_ref.shape[1] // patch_rows
    row_iota = lax.broadcasted_iota(jnp.int32, (patch_rows, lanes), 0)
    col_iota = lax.broadcasted_iota(jnp.int32, (patch_cols, lanes), 0)
    out_ref[...] = jnp.zeros_like(out_ref)

    def step(i, carry):
        base = pl.multiple_of(i * 8, 8)
        ids8 = recv_ref[id_row, pl.ds(base, 8), :].astype(jnp.int32)
        wt = wt_ref[...]
        outs = []
        for g in range(8):
            rows, cols = _split_ids(ids8[g : g + 1, :], shift)
            rhot = (row_iota == rows).astype(BF16)
            rhs = jnp.concatenate([rhot] * parts, axis=0)
            picked = jnp.dot(wt, rhs, preferred_element_type=F32)
            sel = jnp.where(col_iota == cols, picked, 0.0)
            outs.append(jnp.sum(sel, axis=0, keepdims=True))
        rnd = base // owners
        first = pl.multiple_of(base - rnd * owners, 8)
        out_ref[pl.ds(first, 8), rnd, :] = jnp.concatenate(outs, axis=0)
        return carry

    lax.fori_loop(0, count_ref[0] // 8, step, 0)


def gather_field(count, recv, field, owners, capacity):
    patch_rows, patch_cols = field.shape
    shift = patch_cols.bit_length() - 1
    hi = to_bf16_grid(field)
    rest = field - hi
    mid = to_bf16_grid(rest)
    lo = rest - mid
    wt = jnp.concatenate([hi.T, mid.T, lo.T], axis=1).astype(BF16)
    kernel = lambda *refs: _gather_kernel(*refs, patch_rows=patch_rows, shift=shift)
    return pl.pallas_call(
        kernel,
        out_shape=jax.ShapeDtypeStruct((owners, capacity, recv.shape[2]), F32),
        in_specs=[pl.BlockSpec(memory_space=pltpu.SMEM)]
        + [pl.BlockSpec(memory_space=pltpu.VMEM)] * 2,
        out_specs=pl.BlockSpec(memory_space=pltpu.VMEM),
        name="gather_field",
    )(count, recv, wt)


def with_halo(x, width):
    ch, rows, cols = x.shape
    n = lax.axis_size("cells")
    m = lax.axis_size("slab")
    slab = lax.axis_index("slab")
    fwd = [(i, (i + 1) % n) for i in range(n)]
    bwd = [((i + 1) % n, i) for i in range(n)]
    left = lax.ppermute(x[:, :, cols - width :], "cells", fwd)
    right = lax.ppermute(x[:, :, :width], "cells", bwd)
    facing = jnp.where(slab == 0, x[:, rows - width :, :], x[:, :width, :])
    swap = [(j, m - 1 - j) for j in range(m)]
    across = lax.ppermute(facing, "slab", swap)
    sides = jnp.concatenate([left, right], axis=2)
    facing_sides = jnp.where(slab == 0, sides[:, rows - width :, :], sides[:, :width, :])
    corners = lax.ppermute(facing_sides, "slab", swap)
    band = jnp.concatenate([left, x, right], axis=2)
    cap = jnp.concatenate([corners[:, :, :width], across, corners[:, :, width:]], axis=2)
    zero = jnp.zeros_like(cap)
    top = jnp.where(slab == 0, zero, cap)
    bottom = jnp.where(slab == 0, cap, zero)
    return jnp.concatenate([top, band, bottom], axis=1)


def on_device(
    block_owner,
    contact_elem,
    grain_offset,
    grain_vel,
    grain_radius,
    disp_cached,
    wall_disp,
    wall_vel,
    wall_stiff,
):
    owners = lax.axis_size("cells")
    blocks = block_owner.shape[0]
    tile_len = contact_elem.shape[0] // blocks
    patch_rows, patch_cols = wall_stiff.shape
    total_cols = patch_cols * owners
    capacity = 2 * (blocks // owners)
    slots = owners * capacity
    width = SUBSTEPS
    elements = contact_elem.reshape(blocks, tile_len)
    radius_tiles = grain_radius.reshape(blocks, tile_len)
    col_index = block_owner[:, None] * patch_cols + elements % patch_cols
    facing_cos, facing_sin = normals(col_index, total_cols)
    push, reach = contact_push(
        grain_offset.reshape(3, blocks, tile_len),
        grain_vel.reshape(3, blocks, tile_len),
        radius_tiles,
        disp_cached.reshape(3, blocks, tile_len),
        facing_cos,
        facing_sin,
    )
    patches = jnp.arange(owners, dtype=jnp.int32)
    member = (block_owner[:, None] == patches[None, :]).astype(jnp.float32)
    tile_ids = jnp.arange(blocks, dtype=jnp.int32)
    before = (tile_ids[None, :] < tile_ids[:, None]).astype(jnp.float32)
    earlier = jnp.dot(before, member, precision=HIGHEST)
    slot = jnp.sum(earlier * member, axis=1).astype(jnp.int32) * owners + block_owner
    placing = (slot[None, :] == jnp.arange(slots, dtype=jnp.int32)[:, None]).astype(jnp.float32)
    sentinel = patch_rows * patch_cols
    payload = jnp.concatenate([push, elements.astype(jnp.float32)[None]], axis=0)
    send = jnp.einsum("sb,cbl->csl", placing, payload, precision=HIGHEST)
    filled = jnp.sum(placing, axis=1) > 0.5
    send = jnp.concatenate(
        [send[:3], jnp.where(filled[:, None], send[3], float(sentinel))[None]], axis=0
    )
    recv = lax.all_to_all(
        send.reshape(4, capacity, owners, tile_len),
        "cells",
        split_axis=2,
        concat_axis=2,
        tiled=True,
    ).reshape(4, slots, tile_len)
    round_used = jnp.any(recv[3].reshape(capacity, owners * tile_len) < sentinel, axis=1)
    rounds = jnp.max(jnp.where(round_used, jnp.arange(1, capacity + 1, dtype=jnp.int32), 0))
    count = (rounds * owners).reshape(1)

    traction = scatter_traction(count, recv, patch_rows, patch_cols)
    state = jnp.concatenate([wall_disp, wall_vel, wall_stiff[None], traction], axis=0)
    state_ext = with_halo(state, width)
    d_ext, v_ext, stiff_ext = state_ext[:3], state_ext[3:6], state_ext[6]
    traction_ext = state_ext[7:10]

    first_col = lax.axis_index("cells") * patch_cols
    ext_cols = (first_col - width + jnp.arange(patch_cols + 2 * width, dtype=jnp.int32)) % total_cols
    ext_cos, ext_sin = normals(ext_cols, total_cols)
    displace, velocity = (d_ext, v_ext)
    for substep in range(SUBSTEPS):
        padded = jnp.pad(displace, ((0, 0), (1, 1), (0, 0)))
        vertical = padded[:, 2:] + padded[:, :-2]
        padded_c = jnp.pad(displace, ((0, 0), (0, 0), (1, 1)))
        sideways = padded_c[:, :, 2:] + padded_c[:, :, :-2]
        displace, velocity = advance(
            displace, velocity, traction_ext, stiff_ext, vertical, sideways, ext_cos, ext_sin
        )
    wall_next = displace[:, width : width + patch_rows, width : width + patch_cols]
    own_cos = ext_cos[width : width + patch_cols]
    own_sin = ext_sin[width : width + patch_cols]
    radial_field = wall_next[0] * own_cos + wall_next[1] * own_sin
    landed_out = gather_field(count, recv, radial_field, owners, capacity)
    landed_back = lax.all_to_all(
        landed_out, "cells", split_axis=0, concat_axis=0, tiled=True
    ).reshape(slots, tile_len)
    back_slot = block_owner * capacity + jnp.sum(earlier * member, axis=1).astype(jnp.int32)
    taking = (back_slot[None, :] == jnp.arange(slots, dtype=jnp.int32)[:, None]).astype(jnp.float32)
    landed = jnp.einsum("sb,sl->bl", taking, landed_back, precision=HIGHEST)
    contact_gap = radius_tiles + reach - landed
    return (wall_next, contact_gap.reshape(-1))


def solution(mesh):
    return jax.shard_map(
        on_device,
        mesh=mesh,
        in_specs=(
            P(("cells", "slab")),
            P(("cells", "slab")),
            P(None, ("cells", "slab")),
            P(None, ("cells", "slab")),
            P(("cells", "slab")),
            P(None, ("cells", "slab")),
            P(None, "slab", "cells"),
            P(None, "slab", "cells"),
            P("slab", "cells"),
        ),
        out_specs=(P(None, "slab", "cells"), P(("cells", "slab"))),
        check_vma=False,
    )
```

```python
import math

import jax
import jax.numpy as jnp
from jax import lax
from jax.experimental import pallas as pl
from jax.experimental.pallas import tpu as pltpu
from jax.sharding import PartitionSpec as P

SUBSTEPS = 4


SPRING_RATE = 2.0
SOFTNESS = 0.25
APPROACH_DAMP = 0.5
FRICTION = 0.4
SLIP_SPEED = 0.1
HOOP_RATE = 0.5
SHELL_DAMP = 0.3
TIME_STEP = 0.2
FULL_TURN = 2.0 * math.pi
HIGHEST = lax.Precision.HIGHEST
BF16 = jnp.bfloat16
F32 = jnp.float32


def normals(column, total_cols):
    angle = (column.astype(jnp.float32) + 0.5) * (FULL_TURN / total_cols)
    return (jnp.cos(angle), jnp.sin(angle))


def contact_push(offset, velocity, radius, cached, facing_cos, facing_sin):
    reach = offset[0] * facing_cos + offset[1] * facing_sin
    intersection = radius + reach - (cached[0] * facing_cos + cached[1] * facing_sin)
    spring = SPRING_RATE * SOFTNESS * jax.nn.softplus(intersection / SOFTNESS)
    approach = velocity[0] * facing_cos + velocity[1] * facing_sin
    pressing = spring + APPROACH_DAMP * approach
    slide_x = velocity[0] - approach * facing_cos
    slide_y = velocity[1] - approach * facing_sin
    slide_z = velocity[2]
    speed = jnp.sqrt(
        slide_x * slide_x + slide_y * slide_y + slide_z * slide_z + SLIP_SPEED * SLIP_SPEED
    )
    friction = FRICTION * spring / speed
    push = jnp.stack(
        [
            pressing * facing_cos + friction * slide_x,
            pressing * facing_sin + friction * slide_y,
            friction * slide_z,
        ]
    )
    return (push, reach)


def advance(displace, velocity, traction, stiffness, vertical, sideways, facing_cos, facing_sin):
    internal = stiffness * (vertical + sideways - 4.0 * displace)
    radial = HOOP_RATE * stiffness * (displace[0] * facing_cos + displace[1] * facing_sin)
    hoop = jnp.stack([radial * facing_cos, radial * facing_sin, jnp.zeros_like(radial)])
    acceleration = internal - hoop + traction - SHELL_DAMP * velocity
    velocity = velocity + TIME_STEP * acceleration
    return (displace + TIME_STEP * velocity, velocity)


def to_bf16_grid(x):
    return lax.reduce_precision(x, exponent_bits=8, mantissa_bits=7)


def _split_ids(ids, shift):
    rows = lax.shift_right_logical(ids, jnp.int32(shift))
    cols = jnp.bitwise_and(ids, jnp.int32((1 << shift) - 1))
    return rows, cols


def _scatter_kernel(count_ref, recv_ref, out_ref, *, patch_rows, shift):
    comps = recv_ref.shape[0] - 1
    lanes = recv_ref.shape[2]
    patch_cols = 1 << shift
    row_iota = lax.broadcasted_iota(jnp.int32, (patch_rows, lanes), 0)
    col_iota = lax.broadcasted_iota(jnp.int32, (patch_cols, lanes), 0)
    out_ref[...] = jnp.zeros_like(out_ref)

    def step(i, carry):
        base = pl.multiple_of(i * 8, 8)
        blk = recv_ref[:, pl.ds(base, 8), :]
        ids8 = blk[comps].astype(jnp.int32)
        total = None
        for g in range(8):
            rows, cols = _split_ids(ids8[g : g + 1, :], shift)
            rhot = (row_iota == rows).astype(BF16)
            chot = (col_iota == cols).astype(BF16)
            his, los = [], []
            for c in range(comps):
                p = blk[c, g : g + 1, :]
                hi = p.astype(BF16)
                lo = (p - hi.astype(F32)).astype(BF16)
                his.append(rhot * hi)
                los.append(rhot * lo)
            lhs = jnp.concatenate(
                [jnp.concatenate(his, axis=0), jnp.concatenate(los, axis=0)], axis=1
            )
            rhs = jnp.concatenate([chot, chot], axis=1)
            part = lax.dot_general(
                lhs, rhs, (((1,), (1,)), ((), ())), preferred_element_type=F32
            )
            total = part if total is None else total + part
        out_ref[...] += total
        return carry

    lax.fori_loop(0, count_ref[0] // 8, step, 0)


def scatter_traction(count, recv, patch_rows, patch_cols):
    shift = patch_cols.bit_length() - 1
    comps = recv.shape[0] - 1
    kernel = lambda *refs: _scatter_kernel(*refs, patch_rows=patch_rows, shift=shift)
    out = pl.pallas_call(
        kernel,
        out_shape=jax.ShapeDtypeStruct((comps * patch_rows, patch_cols), F32),
        in_specs=[pl.BlockSpec(memory_space=pltpu.SMEM), pl.BlockSpec(memory_space=pltpu.VMEM)],
        out_specs=pl.BlockSpec(memory_space=pltpu.VMEM),
        name="scatter_traction",
    )(count, recv)
    return out.reshape(comps, patch_rows, patch_cols)


def _gather_kernel(count_ref, recv_ref, wt_ref, out_ref, *, patch_rows, shift):
    owners = out_ref.shape[0]
    lanes = recv_ref.shape[2]
    id_row = recv_ref.shape[0] - 1
    patch_cols = 1 << shift
    parts = wt_ref.shape[1] // patch_rows
    row_iota = lax.broadcasted_iota(jnp.int32, (patch_rows, lanes), 0)
    col_iota = lax.broadcasted_iota(jnp.int32, (patch_cols, lanes), 0)
    out_ref[...] = jnp.zeros_like(out_ref)

    def step(i, carry):
        base = pl.multiple_of(i * 8, 8)
        ids8 = recv_ref[id_row, pl.ds(base, 8), :].astype(jnp.int32)
        wt = wt_ref[...]
        outs = []
        for g in range(8):
            rows, cols = _split_ids(ids8[g : g + 1, :], shift)
            rhot = (row_iota == rows).astype(BF16)
            rhs = jnp.concatenate([rhot] * parts, axis=0)
            picked = jnp.dot(wt, rhs, preferred_element_type=F32)
            sel = jnp.where(col_iota == cols, picked, 0.0)
            outs.append(jnp.sum(sel, axis=0, keepdims=True))
        rnd = base // owners
        first = pl.multiple_of(base - rnd * owners, 8)
        out_ref[pl.ds(first, 8), rnd, :] = jnp.concatenate(outs, axis=0)
        return carry

    lax.fori_loop(0, count_ref[0] // 8, step, 0)


def gather_field(count, recv, field, owners, capacity):
    patch_rows, patch_cols = field.shape
    shift = patch_cols.bit_length() - 1
    hi = to_bf16_grid(field)
    rest = field - hi
    mid = to_bf16_grid(rest)
    lo = rest - mid
    wt = jnp.concatenate([hi.T, mid.T, lo.T], axis=1).astype(BF16)
    kernel = lambda *refs: _gather_kernel(*refs, patch_rows=patch_rows, shift=shift)
    return pl.pallas_call(
        kernel,
        out_shape=jax.ShapeDtypeStruct((owners, capacity, recv.shape[2]), F32),
        in_specs=[pl.BlockSpec(memory_space=pltpu.SMEM)]
        + [pl.BlockSpec(memory_space=pltpu.VMEM)] * 2,
        out_specs=pl.BlockSpec(memory_space=pltpu.VMEM),
        name="gather_field",
    )(count, recv, wt)


def with_halo(x, width):
    ch, rows, cols = x.shape
    n = lax.axis_size("cells")
    m = lax.axis_size("slab")
    slab = lax.axis_index("slab")
    fwd = [(i, (i + 1) % n) for i in range(n)]
    bwd = [((i + 1) % n, i) for i in range(n)]
    left = lax.ppermute(x[:, :, cols - width :], "cells", fwd)
    right = lax.ppermute(x[:, :, :width], "cells", bwd)
    facing = jnp.where(slab == 0, x[:, rows - width :, :], x[:, :width, :])
    swap = [(j, m - 1 - j) for j in range(m)]
    across = lax.ppermute(facing, "slab", swap)
    sides = jnp.concatenate([left, right], axis=2)
    facing_sides = jnp.where(slab == 0, sides[:, rows - width :, :], sides[:, :width, :])
    corners = lax.ppermute(facing_sides, "slab", swap)
    band = jnp.concatenate([left, x, right], axis=2)
    cap = jnp.concatenate([corners[:, :, :width], across, corners[:, :, width:]], axis=2)
    zero = jnp.zeros_like(cap)
    top = jnp.where(slab == 0, zero, cap)
    bottom = jnp.where(slab == 0, cap, zero)
    return jnp.concatenate([top, band, bottom], axis=1)


def on_device(
    block_owner,
    contact_elem,
    grain_offset,
    grain_vel,
    grain_radius,
    disp_cached,
    wall_disp,
    wall_vel,
    wall_stiff,
):
    owners = lax.axis_size("cells")
    blocks = block_owner.shape[0]
    tile_len = contact_elem.shape[0] // blocks
    patch_rows, patch_cols = wall_stiff.shape
    total_cols = patch_cols * owners
    capacity = 2 * (blocks // owners)
    slots = owners * capacity
    width = SUBSTEPS
    elements = contact_elem.reshape(blocks, tile_len)
    radius_tiles = grain_radius.reshape(blocks, tile_len)
    col_index = block_owner[:, None] * patch_cols + elements % patch_cols
    facing_cos, facing_sin = normals(col_index, total_cols)
    push, reach = contact_push(
        grain_offset.reshape(3, blocks, tile_len),
        grain_vel.reshape(3, blocks, tile_len),
        radius_tiles,
        disp_cached.reshape(3, blocks, tile_len),
        facing_cos,
        facing_sin,
    )
    patches = jnp.arange(owners, dtype=jnp.int32)
    member = (block_owner[:, None] == patches[None, :]).astype(jnp.float32)
    tile_ids = jnp.arange(blocks, dtype=jnp.int32)
    before = (tile_ids[None, :] < tile_ids[:, None]).astype(jnp.float32)
    earlier = jnp.dot(before, member, precision=HIGHEST)
    slot = jnp.sum(earlier * member, axis=1).astype(jnp.int32) * owners + block_owner
    placing = (slot[None, :] == jnp.arange(slots, dtype=jnp.int32)[:, None]).astype(jnp.float32)
    sentinel = patch_rows * patch_cols
    payload = jnp.concatenate([push, elements.astype(jnp.float32)[None]], axis=0)
    send = jnp.einsum("sb,cbl->csl", placing, payload, precision=HIGHEST)
    filled = jnp.sum(placing, axis=1) > 0.5
    send = jnp.concatenate(
        [send[:3], jnp.where(filled[:, None], send[3], float(sentinel))[None]], axis=0
    )
    recv = lax.all_to_all(
        send.reshape(4, capacity, owners, tile_len),
        "cells",
        split_axis=2,
        concat_axis=2,
        tiled=True,
    ).reshape(4, slots, tile_len)
    round_used = jnp.any(recv[3].reshape(capacity, owners * tile_len) < sentinel, axis=1)
    rounds = jnp.max(jnp.where(round_used, jnp.arange(1, capacity + 1, dtype=jnp.int32), 0))
    count = (rounds * owners).reshape(1)

    traction = scatter_traction(count, recv, patch_rows, patch_cols)
    state = jnp.concatenate([wall_disp, wall_vel, wall_stiff[None], traction], axis=0)
    state_ext = with_halo(state, width)
    d_ext, v_ext, stiff_ext = state_ext[:3], state_ext[3:6], state_ext[6]
    traction_ext = state_ext[7:10]

    first_col = lax.axis_index("cells") * patch_cols
    ext_cols = (first_col - width + jnp.arange(patch_cols + 2 * width, dtype=jnp.int32)) % total_cols
    ext_cos, ext_sin = normals(ext_cols, total_cols)
    displace, velocity = (d_ext, v_ext)
    for substep in range(SUBSTEPS):
        padded = jnp.pad(displace, ((0, 0), (1, 1), (0, 0)))
        vertical = padded[:, 2:] + padded[:, :-2]
        padded_c = jnp.pad(displace, ((0, 0), (0, 0), (1, 1)))
        sideways = padded_c[:, :, 2:] + padded_c[:, :, :-2]
        displace, velocity = advance(
            displace, velocity, traction_ext, stiff_ext, vertical, sideways, ext_cos, ext_sin
        )
    wall_next = displace[:, width : width + patch_rows, width : width + patch_cols]
    own_cos = ext_cos[width : width + patch_cols]
    own_sin = ext_sin[width : width + patch_cols]
    radial_field = wall_next[0] * own_cos + wall_next[1] * own_sin
    landed_out = gather_field(count, recv, radial_field, owners, capacity)
    landed_back = lax.all_to_all(
        landed_out, "cells", split_axis=0, concat_axis=0, tiled=True
    ).reshape(slots, tile_len)
    back_slot = block_owner * capacity + jnp.sum(earlier * member, axis=1).astype(jnp.int32)
    landed = jnp.take(landed_back, back_slot, axis=0, mode="clip")
    contact_gap = radius_tiles + reach - landed
    return (wall_next, contact_gap.reshape(-1))


def solution(mesh):
    return jax.shard_map(
        on_device,
        mesh=mesh,
        in_specs=(
            P(("cells", "slab")),
            P(("cells", "slab")),
            P(None, ("cells", "slab")),
            P(None, ("cells", "slab")),
            P(("cells", "slab")),
            P(None, ("cells", "slab")),
            P(None, "slab", "cells"),
            P(None, "slab", "cells"),
            P("slab", "cells"),
        ),
        out_specs=(P(None, "slab", "cells"), P(("cells", "slab"))),
        check_vma=False,
    )
```

```python
import math

import jax
import jax.numpy as jnp
from jax import lax
from jax.experimental import pallas as pl
from jax.experimental.pallas import tpu as pltpu
from jax.sharding import PartitionSpec as P

SUBSTEPS = 4


SPRING_RATE = 2.0
SOFTNESS = 0.25
APPROACH_DAMP = 0.5
FRICTION = 0.4
SLIP_SPEED = 0.1
HOOP_RATE = 0.5
SHELL_DAMP = 0.3
TIME_STEP = 0.2
FULL_TURN = 2.0 * math.pi
HIGHEST = lax.Precision.HIGHEST
BF16 = jnp.bfloat16
F32 = jnp.float32


def normals(column, total_cols):
    angle = (column.astype(jnp.float32) + 0.5) * (FULL_TURN / total_cols)
    return (jnp.cos(angle), jnp.sin(angle))


def contact_push(offset, velocity, radius, cached, facing_cos, facing_sin):
    reach = offset[0] * facing_cos + offset[1] * facing_sin
    intersection = radius + reach - (cached[0] * facing_cos + cached[1] * facing_sin)
    spring = SPRING_RATE * SOFTNESS * jax.nn.softplus(intersection / SOFTNESS)
    approach = velocity[0] * facing_cos + velocity[1] * facing_sin
    pressing = spring + APPROACH_DAMP * approach
    slide_x = velocity[0] - approach * facing_cos
    slide_y = velocity[1] - approach * facing_sin
    slide_z = velocity[2]
    speed = jnp.sqrt(
        slide_x * slide_x + slide_y * slide_y + slide_z * slide_z + SLIP_SPEED * SLIP_SPEED
    )
    friction = FRICTION * spring / speed
    push = jnp.stack(
        [
            pressing * facing_cos + friction * slide_x,
            pressing * facing_sin + friction * slide_y,
            friction * slide_z,
        ]
    )
    return (push, reach)


def advance(displace, velocity, traction, stiffness, vertical, sideways, facing_cos, facing_sin):
    internal = stiffness * (vertical + sideways - 4.0 * displace)
    radial = HOOP_RATE * stiffness * (displace[0] * facing_cos + displace[1] * facing_sin)
    hoop = jnp.stack([radial * facing_cos, radial * facing_sin, jnp.zeros_like(radial)])
    acceleration = internal - hoop + traction - SHELL_DAMP * velocity
    velocity = velocity + TIME_STEP * acceleration
    return (displace + TIME_STEP * velocity, velocity)


def to_bf16_grid(x):
    return lax.reduce_precision(x, exponent_bits=8, mantissa_bits=7)


def _split_ids(ids, shift):
    rows = lax.shift_right_logical(ids, jnp.int32(shift))
    cols = jnp.bitwise_and(ids, jnp.int32((1 << shift) - 1))
    return rows, cols


def _scatter_kernel(count_ref, recv_ref, out_ref, *, patch_rows, shift):
    comps = recv_ref.shape[0] - 1
    lanes = recv_ref.shape[2]
    patch_cols = 1 << shift
    row_iota = lax.broadcasted_iota(jnp.int32, (patch_rows, lanes), 0)
    col_iota = lax.broadcasted_iota(jnp.int32, (patch_cols, lanes), 0)
    out_ref[...] = jnp.zeros_like(out_ref)

    def step(i, carry):
        base = pl.multiple_of(i * 8, 8)
        blk = recv_ref[:, pl.ds(base, 8), :]
        ids8 = blk[comps].astype(jnp.int32)
        total = None
        for g in range(8):
            rows, cols = _split_ids(ids8[g : g + 1, :], shift)
            rhot = (row_iota == rows).astype(BF16)
            chot = (col_iota == cols).astype(BF16)
            his, los = [], []
            for c in range(comps):
                p = blk[c, g : g + 1, :]
                hi = p.astype(BF16)
                lo = (p - hi.astype(F32)).astype(BF16)
                his.append(rhot * hi)
                los.append(rhot * lo)
            lhs = jnp.concatenate(
                [jnp.concatenate(his, axis=0), jnp.concatenate(los, axis=0)], axis=1
            )
            rhs = jnp.concatenate([chot, chot], axis=1)
            part = lax.dot_general(
                lhs, rhs, (((1,), (1,)), ((), ())), preferred_element_type=F32
            )
            total = part if total is None else total + part
        out_ref[...] += total
        return carry

    lax.fori_loop(0, count_ref[0] // 8, step, 0)


def scatter_traction(count, recv, patch_rows, patch_cols):
    shift = patch_cols.bit_length() - 1
    comps = recv.shape[0] - 1
    kernel = lambda *refs: _scatter_kernel(*refs, patch_rows=patch_rows, shift=shift)
    out = pl.pallas_call(
        kernel,
        out_shape=jax.ShapeDtypeStruct((comps * patch_rows, patch_cols), F32),
        in_specs=[pl.BlockSpec(memory_space=pltpu.SMEM), pl.BlockSpec(memory_space=pltpu.VMEM)],
        out_specs=pl.BlockSpec(memory_space=pltpu.VMEM),
        name="scatter_traction",
    )(count, recv)
    return out.reshape(comps, patch_rows, patch_cols)


def _gather_kernel(count_ref, recv_ref, wt_ref, out_ref, *, patch_rows, shift):
    owners = out_ref.shape[0]
    lanes = recv_ref.shape[2]
    id_row = recv_ref.shape[0] - 1
    patch_cols = 1 << shift
    parts = wt_ref.shape[1] // patch_rows
    row_iota = lax.broadcasted_iota(jnp.int32, (patch_rows, lanes), 0)
    col_iota = lax.broadcasted_iota(jnp.int32, (patch_cols, lanes), 0)
    out_ref[...] = jnp.zeros_like(out_ref)

    def step(i, carry):
        base = pl.multiple_of(i * 8, 8)
        ids8 = recv_ref[id_row, pl.ds(base, 8), :].astype(jnp.int32)
        wt = wt_ref[...]
        outs = []
        for g in range(8):
            rows, cols = _split_ids(ids8[g : g + 1, :], shift)
            rhot = (row_iota == rows).astype(BF16)
            rhs = jnp.concatenate([rhot] * parts, axis=0)
            picked = jnp.dot(wt, rhs, preferred_element_type=F32)
            sel = jnp.where(col_iota == cols, picked, 0.0)
            outs.append(jnp.sum(sel, axis=0, keepdims=True))
        rnd = base // owners
        first = pl.multiple_of(base - rnd * owners, 8)
        out_ref[pl.ds(first, 8), rnd, :] = jnp.concatenate(outs, axis=0)
        return carry

    lax.fori_loop(0, count_ref[0] // 8, step, 0)


def gather_field(count, recv, field, owners, capacity):
    patch_rows, patch_cols = field.shape
    shift = patch_cols.bit_length() - 1
    hi = to_bf16_grid(field)
    rest = field - hi
    mid = to_bf16_grid(rest)
    lo = rest - mid
    wt = jnp.concatenate([hi.T, mid.T, lo.T], axis=1).astype(BF16)
    kernel = lambda *refs: _gather_kernel(*refs, patch_rows=patch_rows, shift=shift)
    return pl.pallas_call(
        kernel,
        out_shape=jax.ShapeDtypeStruct((owners, capacity, recv.shape[2]), F32),
        in_specs=[pl.BlockSpec(memory_space=pltpu.SMEM)]
        + [pl.BlockSpec(memory_space=pltpu.VMEM)] * 2,
        out_specs=pl.BlockSpec(memory_space=pltpu.VMEM),
        name="gather_field",
    )(count, recv, wt)


def with_halo(x, width):
    ch, rows, cols = x.shape
    n = lax.axis_size("cells")
    m = lax.axis_size("slab")
    slab = lax.axis_index("slab")
    fwd = [(i, (i + 1) % n) for i in range(n)]
    bwd = [((i + 1) % n, i) for i in range(n)]
    left = lax.ppermute(x[:, :, cols - width :], "cells", fwd)
    right = lax.ppermute(x[:, :, :width], "cells", bwd)
    facing = jnp.where(slab == 0, x[:, rows - width :, :], x[:, :width, :])
    swap = [(j, m - 1 - j) for j in range(m)]
    across = lax.ppermute(facing, "slab", swap)
    sides = jnp.concatenate([left, right], axis=2)
    facing_sides = jnp.where(slab == 0, sides[:, rows - width :, :], sides[:, :width, :])
    corners = lax.ppermute(facing_sides, "slab", swap)
    band = jnp.concatenate([left, x, right], axis=2)
    cap = jnp.concatenate([corners[:, :, :width], across, corners[:, :, width:]], axis=2)
    zero = jnp.zeros_like(cap)
    top = jnp.where(slab == 0, zero, cap)
    bottom = jnp.where(slab == 0, cap, zero)
    return jnp.concatenate([top, band, bottom], axis=1)


def on_device(
    block_owner,
    contact_elem,
    grain_offset,
    grain_vel,
    grain_radius,
    disp_cached,
    wall_disp,
    wall_vel,
    wall_stiff,
):
    owners = lax.axis_size("cells")
    blocks = block_owner.shape[0]
    tile_len = contact_elem.shape[0] // blocks
    patch_rows, patch_cols = wall_stiff.shape
    total_cols = patch_cols * owners
    capacity = 2 * (blocks // owners)
    slots = owners * capacity
    width = SUBSTEPS
    elements = contact_elem.reshape(blocks, tile_len)
    radius_tiles = grain_radius.reshape(blocks, tile_len)
    col_index = block_owner[:, None] * patch_cols + elements % patch_cols
    facing_cos, facing_sin = normals(col_index, total_cols)
    push, reach = contact_push(
        grain_offset.reshape(3, blocks, tile_len),
        grain_vel.reshape(3, blocks, tile_len),
        radius_tiles,
        disp_cached.reshape(3, blocks, tile_len),
        facing_cos,
        facing_sin,
    )
    patches = jnp.arange(owners, dtype=jnp.int32)
    member = (block_owner[:, None] == patches[None, :]).astype(jnp.float32)
    tile_ids = jnp.arange(blocks, dtype=jnp.int32)
    before = (tile_ids[None, :] < tile_ids[:, None]).astype(jnp.float32)
    earlier = jnp.dot(before, member, precision=HIGHEST)
    slot = jnp.sum(earlier * member, axis=1).astype(jnp.int32) * owners + block_owner
    placing = (slot[None, :] == jnp.arange(slots, dtype=jnp.int32)[:, None]).astype(jnp.float32)
    sentinel = patch_rows * patch_cols
    payload = jnp.concatenate([push, elements.astype(jnp.float32)[None]], axis=0)
    send = jnp.einsum("sb,cbl->csl", placing, payload, precision=HIGHEST)
    filled = jnp.sum(placing, axis=1) > 0.5
    send = jnp.concatenate(
        [send[:3], jnp.where(filled[:, None], send[3], float(sentinel))[None]], axis=0
    )
    recv = lax.all_to_all(
        send.reshape(4, capacity, owners, tile_len),
        "cells",
        split_axis=2,
        concat_axis=2,
        tiled=True,
    ).reshape(4, slots, tile_len)
    mine = lax.axis_index("cells")
    named = jnp.sum((block_owner == mine).astype(jnp.int32))
    rounds = jnp.clip(named, 1, capacity)
    count = (rounds * owners).reshape(1)

    traction = scatter_traction(count, recv, patch_rows, patch_cols)
    state = jnp.concatenate([wall_disp, wall_vel, wall_stiff[None], traction], axis=0)
    state_ext = with_halo(state, width)
    d_ext, v_ext, stiff_ext = state_ext[:3], state_ext[3:6], state_ext[6]
    traction_ext = state_ext[7:10]

    first_col = lax.axis_index("cells") * patch_cols
    ext_cols = (first_col - width + jnp.arange(patch_cols + 2 * width, dtype=jnp.int32)) % total_cols
    ext_cos, ext_sin = normals(ext_cols, total_cols)
    displace, velocity = (d_ext, v_ext)
    for substep in range(SUBSTEPS):
        padded = jnp.pad(displace, ((0, 0), (1, 1), (0, 0)))
        vertical = padded[:, 2:] + padded[:, :-2]
        padded_c = jnp.pad(displace, ((0, 0), (0, 0), (1, 1)))
        sideways = padded_c[:, :, 2:] + padded_c[:, :, :-2]
        displace, velocity = advance(
            displace, velocity, traction_ext, stiff_ext, vertical, sideways, ext_cos, ext_sin
        )
    wall_next = displace[:, width : width + patch_rows, width : width + patch_cols]
    own_cos = ext_cos[width : width + patch_cols]
    own_sin = ext_sin[width : width + patch_cols]
    radial_field = wall_next[0] * own_cos + wall_next[1] * own_sin
    landed_out = gather_field(count, recv, radial_field, owners, capacity)
    landed_back = lax.all_to_all(
        landed_out, "cells", split_axis=0, concat_axis=0, tiled=True
    ).reshape(slots, tile_len)
    back_slot = block_owner * capacity + jnp.sum(earlier * member, axis=1).astype(jnp.int32)
    taking = (back_slot[None, :] == jnp.arange(slots, dtype=jnp.int32)[:, None]).astype(jnp.float32)
    landed = jnp.einsum("sb,sl->bl", taking, landed_back, precision=HIGHEST)
    contact_gap = radius_tiles + reach - landed
    return (wall_next, contact_gap.reshape(-1))


def solution(mesh):
    return jax.shard_map(
        on_device,
        mesh=mesh,
        in_specs=(
            P(("cells", "slab")),
            P(("cells", "slab")),
            P(None, ("cells", "slab")),
            P(None, ("cells", "slab")),
            P(("cells", "slab")),
            P(None, ("cells", "slab")),
            P(None, "slab", "cells"),
            P(None, "slab", "cells"),
            P("slab", "cells"),
        ),
        out_specs=(P(None, "slab", "cells"), P(("cells", "slab"))),
        check_vma=False,
    )
```

```python
import math

import jax
import jax.numpy as jnp
from jax import lax
from jax.experimental import pallas as pl
from jax.experimental.pallas import tpu as pltpu
from jax.sharding import PartitionSpec as P

SUBSTEPS = 4


SPRING_RATE = 2.0
SOFTNESS = 0.25
APPROACH_DAMP = 0.5
FRICTION = 0.4
SLIP_SPEED = 0.1
HOOP_RATE = 0.5
SHELL_DAMP = 0.3
TIME_STEP = 0.2
FULL_TURN = 2.0 * math.pi
HIGHEST = lax.Precision.HIGHEST
BF16 = jnp.bfloat16
F32 = jnp.float32


def normals(column, total_cols):
    angle = (column.astype(jnp.float32) + 0.5) * (FULL_TURN / total_cols)
    return (jnp.cos(angle), jnp.sin(angle))


def contact_push(offset, velocity, radius, cached, facing_cos, facing_sin):
    reach = offset[0] * facing_cos + offset[1] * facing_sin
    intersection = radius + reach - (cached[0] * facing_cos + cached[1] * facing_sin)
    spring = SPRING_RATE * SOFTNESS * jax.nn.softplus(intersection / SOFTNESS)
    approach = velocity[0] * facing_cos + velocity[1] * facing_sin
    pressing = spring + APPROACH_DAMP * approach
    slide_x = velocity[0] - approach * facing_cos
    slide_y = velocity[1] - approach * facing_sin
    slide_z = velocity[2]
    speed = jnp.sqrt(
        slide_x * slide_x + slide_y * slide_y + slide_z * slide_z + SLIP_SPEED * SLIP_SPEED
    )
    friction = FRICTION * spring / speed
    push = jnp.stack(
        [
            pressing * facing_cos + friction * slide_x,
            pressing * facing_sin + friction * slide_y,
            friction * slide_z,
        ]
    )
    return (push, reach)


def advance(displace, velocity, traction, stiffness, vertical, sideways, facing_cos, facing_sin):
    internal = stiffness * (vertical + sideways - 4.0 * displace)
    radial = HOOP_RATE * stiffness * (displace[0] * facing_cos + displace[1] * facing_sin)
    hoop = jnp.stack([radial * facing_cos, radial * facing_sin, jnp.zeros_like(radial)])
    acceleration = internal - hoop + traction - SHELL_DAMP * velocity
    velocity = velocity + TIME_STEP * acceleration
    return (displace + TIME_STEP * velocity, velocity)


def to_bf16_grid(x):
    return lax.reduce_precision(x, exponent_bits=8, mantissa_bits=7)


def _split_ids(ids, shift):
    rows = lax.shift_right_logical(ids, jnp.int32(shift))
    cols = jnp.bitwise_and(ids, jnp.int32((1 << shift) - 1))
    return rows, cols


def _scatter_kernel(count_ref, recv_ref, out_ref, *, patch_rows, shift, comps):
    owners, _, lanes = recv_ref.shape
    patch_cols = 1 << shift
    width = comps + 1
    row_iota = lax.broadcasted_iota(jnp.int32, (patch_rows, lanes), 0)
    col_iota = lax.broadcasted_iota(jnp.int32, (patch_cols, lanes), 0)
    out_ref[...] = jnp.zeros_like(out_ref)

    def make_step(rnd):
        def step(i, carry):
            base = pl.multiple_of(i * 8, 8)
            blk = recv_ref[pl.ds(base, 8), :, :]
            total = None
            for g in range(8):
                ids = blk[g, rnd * width + comps : rnd * width + comps + 1, :].astype(jnp.int32)
                rows, cols = _split_ids(ids, shift)
                rhot = (row_iota == rows).astype(BF16)
                chot = (col_iota == cols).astype(BF16)
                his, los = [], []
                for c in range(comps):
                    p = blk[g, rnd * width + c : rnd * width + c + 1, :]
                    hi = p.astype(BF16)
                    lo = (p - hi.astype(F32)).astype(BF16)
                    his.append(rhot * hi)
                    los.append(rhot * lo)
                lhs = jnp.concatenate(
                    [jnp.concatenate(his, axis=0), jnp.concatenate(los, axis=0)], axis=1
                )
                rhs = jnp.concatenate([chot, chot], axis=1)
                part = lax.dot_general(
                    lhs, rhs, (((1,), (1,)), ((), ())), preferred_element_type=F32
                )
                total = part if total is None else total + part
            out_ref[...] += total
            return carry

        return step

    capacity = recv_ref.shape[1] // width
    for rnd in range(capacity):
        trips = jnp.clip(count_ref[0] - rnd * owners, 0, owners) // 8
        lax.fori_loop(0, trips, make_step(rnd), 0)


def scatter_traction(count, recv, patch_rows, patch_cols, comps):
    shift = patch_cols.bit_length() - 1
    kernel = lambda *refs: _scatter_kernel(*refs, patch_rows=patch_rows, shift=shift, comps=comps)
    out = pl.pallas_call(
        kernel,
        out_shape=jax.ShapeDtypeStruct((comps * patch_rows, patch_cols), F32),
        in_specs=[pl.BlockSpec(memory_space=pltpu.SMEM), pl.BlockSpec(memory_space=pltpu.VMEM)],
        out_specs=pl.BlockSpec(memory_space=pltpu.VMEM),
        name="scatter_traction",
    )(count, recv)
    return out.reshape(comps, patch_rows, patch_cols)


def _gather_kernel(count_ref, recv_ref, wt_ref, out_ref, *, patch_rows, shift, width):
    owners, capacity, lanes = out_ref.shape
    patch_cols = 1 << shift
    parts = wt_ref.shape[1] // patch_rows
    row_iota = lax.broadcasted_iota(jnp.int32, (patch_rows, lanes), 0)
    col_iota = lax.broadcasted_iota(jnp.int32, (patch_cols, lanes), 0)
    out_ref[...] = jnp.zeros_like(out_ref)

    def make_step(rnd):
        def step(i, carry):
            base = pl.multiple_of(i * 8, 8)
            blk = recv_ref[pl.ds(base, 8), :, :]
            wt = wt_ref[...]
            outs = []
            for g in range(8):
                ids = blk[g, rnd * width + width - 1 : rnd * width + width, :].astype(jnp.int32)
                rows, cols = _split_ids(ids, shift)
                rhot = (row_iota == rows).astype(BF16)
                rhs = jnp.concatenate([rhot] * parts, axis=0)
                picked = jnp.dot(wt, rhs, preferred_element_type=F32)
                sel = jnp.where(col_iota == cols, picked, 0.0)
                outs.append(jnp.sum(sel, axis=0, keepdims=True))
            out_ref[pl.ds(base, 8), rnd, :] = jnp.concatenate(outs, axis=0)
            return carry

        return step

    for rnd in range(capacity):
        trips = jnp.clip(count_ref[0] - rnd * owners, 0, owners) // 8
        lax.fori_loop(0, trips, make_step(rnd), 0)


def gather_field(count, recv, field, owners, capacity):
    patch_rows, patch_cols = field.shape
    shift = patch_cols.bit_length() - 1
    hi = to_bf16_grid(field)
    rest = field - hi
    mid = to_bf16_grid(rest)
    lo = rest - mid
    wt = jnp.concatenate([hi.T, mid.T, lo.T], axis=1).astype(BF16)
    width = recv.shape[1] // capacity
    kernel = lambda *refs: _gather_kernel(*refs, patch_rows=patch_rows, shift=shift, width=width)
    return pl.pallas_call(
        kernel,
        out_shape=jax.ShapeDtypeStruct((owners, capacity, recv.shape[2]), F32),
        in_specs=[pl.BlockSpec(memory_space=pltpu.SMEM)]
        + [pl.BlockSpec(memory_space=pltpu.VMEM)] * 2,
        out_specs=pl.BlockSpec(memory_space=pltpu.VMEM),
        name="gather_field",
    )(count, recv, wt)


def with_halo(x, width):
    ch, rows, cols = x.shape
    n = lax.axis_size("cells")
    m = lax.axis_size("slab")
    slab = lax.axis_index("slab")
    fwd = [(i, (i + 1) % n) for i in range(n)]
    bwd = [((i + 1) % n, i) for i in range(n)]
    left = lax.ppermute(x[:, :, cols - width :], "cells", fwd)
    right = lax.ppermute(x[:, :, :width], "cells", bwd)
    facing = jnp.where(slab == 0, x[:, rows - width :, :], x[:, :width, :])
    swap = [(j, m - 1 - j) for j in range(m)]
    across = lax.ppermute(facing, "slab", swap)
    sides = jnp.concatenate([left, right], axis=2)
    facing_sides = jnp.where(slab == 0, sides[:, rows - width :, :], sides[:, :width, :])
    corners = lax.ppermute(facing_sides, "slab", swap)
    band = jnp.concatenate([left, x, right], axis=2)
    cap = jnp.concatenate([corners[:, :, :width], across, corners[:, :, width:]], axis=2)
    zero = jnp.zeros_like(cap)
    top = jnp.where(slab == 0, zero, cap)
    bottom = jnp.where(slab == 0, cap, zero)
    return jnp.concatenate([top, band, bottom], axis=1)


def on_device(
    block_owner,
    contact_elem,
    grain_offset,
    grain_vel,
    grain_radius,
    disp_cached,
    wall_disp,
    wall_vel,
    wall_stiff,
):
    owners = lax.axis_size("cells")
    blocks = block_owner.shape[0]
    tile_len = contact_elem.shape[0] // blocks
    patch_rows, patch_cols = wall_stiff.shape
    total_cols = patch_cols * owners
    capacity = 2 * (blocks // owners)
    slots = owners * capacity
    width = SUBSTEPS
    elements = contact_elem.reshape(blocks, tile_len)
    radius_tiles = grain_radius.reshape(blocks, tile_len)
    col_index = block_owner[:, None] * patch_cols + elements % patch_cols
    facing_cos, facing_sin = normals(col_index, total_cols)
    push, reach = contact_push(
        grain_offset.reshape(3, blocks, tile_len),
        grain_vel.reshape(3, blocks, tile_len),
        radius_tiles,
        disp_cached.reshape(3, blocks, tile_len),
        facing_cos,
        facing_sin,
    )
    patches = jnp.arange(owners, dtype=jnp.int32)
    member = (block_owner[:, None] == patches[None, :]).astype(jnp.float32)
    tile_ids = jnp.arange(blocks, dtype=jnp.int32)
    before = (tile_ids[None, :] < tile_ids[:, None]).astype(jnp.float32)
    earlier = jnp.dot(before, member, precision=HIGHEST)
    slot = jnp.sum(earlier * member, axis=1).astype(jnp.int32) * owners + block_owner
    placing = (slot[None, :] == jnp.arange(slots, dtype=jnp.int32)[:, None]).astype(jnp.float32)
    sentinel = patch_rows * patch_cols
    payload = jnp.concatenate([push, elements.astype(jnp.float32)[None]], axis=0)
    send = jnp.einsum("sb,cbl->csl", placing, payload, precision=HIGHEST)
    filled = jnp.sum(placing, axis=1) > 0.5
    send = jnp.concatenate(
        [send[:3], jnp.where(filled[:, None], send[3], float(sentinel))[None]], axis=0
    )
    send = jnp.transpose(send.reshape(4, capacity, owners, tile_len), (2, 1, 0, 3))
    recv = lax.all_to_all(
        send.reshape(owners, capacity * 4, tile_len),
        "cells",
        split_axis=0,
        concat_axis=0,
        tiled=True,
    )
    mine = lax.axis_index("cells")
    named = jnp.sum((block_owner == mine).astype(jnp.int32))
    rounds = jnp.clip(named, 1, capacity)
    count = (rounds * owners).reshape(1)

    traction = scatter_traction(count, recv, patch_rows, patch_cols, 3)
    state = jnp.concatenate([wall_disp, wall_vel, wall_stiff[None], traction], axis=0)
    state_ext = with_halo(state, width)
    d_ext, v_ext, stiff_ext = state_ext[:3], state_ext[3:6], state_ext[6]
    traction_ext = state_ext[7:10]

    first_col = lax.axis_index("cells") * patch_cols
    ext_cols = (first_col - width + jnp.arange(patch_cols + 2 * width, dtype=jnp.int32)) % total_cols
    ext_cos, ext_sin = normals(ext_cols, total_cols)
    displace, velocity = (d_ext, v_ext)
    for substep in range(SUBSTEPS):
        padded = jnp.pad(displace, ((0, 0), (1, 1), (0, 0)))
        vertical = padded[:, 2:] + padded[:, :-2]
        padded_c = jnp.pad(displace, ((0, 0), (0, 0), (1, 1)))
        sideways = padded_c[:, :, 2:] + padded_c[:, :, :-2]
        displace, velocity = advance(
            displace, velocity, traction_ext, stiff_ext, vertical, sideways, ext_cos, ext_sin
        )
    wall_next = displace[:, width : width + patch_rows, width : width + patch_cols]
    own_cos = ext_cos[width : width + patch_cols]
    own_sin = ext_sin[width : width + patch_cols]
    radial_field = wall_next[0] * own_cos + wall_next[1] * own_sin
    landed_out = gather_field(count, recv, radial_field, owners, capacity)
    landed_back = lax.all_to_all(
        landed_out, "cells", split_axis=0, concat_axis=0, tiled=True
    ).reshape(slots, tile_len)
    back_slot = block_owner * capacity + jnp.sum(earlier * member, axis=1).astype(jnp.int32)
    taking = (back_slot[None, :] == jnp.arange(slots, dtype=jnp.int32)[:, None]).astype(jnp.float32)
    landed = jnp.einsum("sb,sl->bl", taking, landed_back, precision=HIGHEST)
    contact_gap = radius_tiles + reach - landed
    return (wall_next, contact_gap.reshape(-1))


def solution(mesh):
    return jax.shard_map(
        on_device,
        mesh=mesh,
        in_specs=(
            P(("cells", "slab")),
            P(("cells", "slab")),
            P(None, ("cells", "slab")),
            P(None, ("cells", "slab")),
            P(("cells", "slab")),
            P(None, ("cells", "slab")),
            P(None, "slab", "cells"),
            P(None, "slab", "cells"),
            P("slab", "cells"),
        ),
        out_specs=(P(None, "slab", "cells"), P(("cells", "slab"))),
        check_vma=False,
    )
```

```python
import math

import jax
import jax.numpy as jnp
from jax import lax
from jax.experimental import pallas as pl
from jax.experimental.pallas import tpu as pltpu
from jax.sharding import PartitionSpec as P

SUBSTEPS = 4


SPRING_RATE = 2.0
SOFTNESS = 0.25
APPROACH_DAMP = 0.5
FRICTION = 0.4
SLIP_SPEED = 0.1
HOOP_RATE = 0.5
SHELL_DAMP = 0.3
TIME_STEP = 0.2
FULL_TURN = 2.0 * math.pi
HIGHEST = lax.Precision.HIGHEST
BF16 = jnp.bfloat16
F32 = jnp.float32


def normals(column, total_cols):
    angle = (column.astype(jnp.float32) + 0.5) * (FULL_TURN / total_cols)
    return (jnp.cos(angle), jnp.sin(angle))


def contact_push(offset, velocity, radius, cached, facing_cos, facing_sin):
    reach = offset[0] * facing_cos + offset[1] * facing_sin
    intersection = radius + reach - (cached[0] * facing_cos + cached[1] * facing_sin)
    spring = SPRING_RATE * SOFTNESS * jax.nn.softplus(intersection / SOFTNESS)
    approach = velocity[0] * facing_cos + velocity[1] * facing_sin
    pressing = spring + APPROACH_DAMP * approach
    slide_x = velocity[0] - approach * facing_cos
    slide_y = velocity[1] - approach * facing_sin
    slide_z = velocity[2]
    speed = jnp.sqrt(
        slide_x * slide_x + slide_y * slide_y + slide_z * slide_z + SLIP_SPEED * SLIP_SPEED
    )
    friction = FRICTION * spring / speed
    push = jnp.stack(
        [
            pressing * facing_cos + friction * slide_x,
            pressing * facing_sin + friction * slide_y,
            friction * slide_z,
        ]
    )
    return (push, reach)


def advance(displace, velocity, traction, stiffness, vertical, sideways, facing_cos, facing_sin):
    internal = stiffness * (vertical + sideways - 4.0 * displace)
    radial = HOOP_RATE * stiffness * (displace[0] * facing_cos + displace[1] * facing_sin)
    hoop = jnp.stack([radial * facing_cos, radial * facing_sin, jnp.zeros_like(radial)])
    acceleration = internal - hoop + traction - SHELL_DAMP * velocity
    velocity = velocity + TIME_STEP * acceleration
    return (displace + TIME_STEP * velocity, velocity)


def to_bf16_grid(x):
    return lax.reduce_precision(x, exponent_bits=8, mantissa_bits=7)


def _split_ids(ids, shift):
    rows = lax.shift_right_logical(ids, jnp.int32(shift))
    cols = jnp.bitwise_and(ids, jnp.int32((1 << shift) - 1))
    return rows, cols


def _scatter_kernel(count_ref, recv_ref, out_ref, *, patch_rows, shift, comps):
    owners, _, lanes = recv_ref.shape
    patch_cols = 1 << shift
    width = comps + 1
    row_iota = lax.broadcasted_iota(jnp.int32, (patch_rows, lanes), 0)
    col_iota = lax.broadcasted_iota(jnp.int32, (patch_cols, lanes), 0)
    out_ref[...] = jnp.zeros_like(out_ref)

    def make_step(rnd):
        def step(i, carry):
            base = pl.multiple_of(i * 8, 8)
            blk = recv_ref[pl.ds(base, 8), :, :]
            total = None
            for g in range(8):
                ids = blk[g, rnd * width + comps : rnd * width + comps + 1, :].astype(jnp.int32)
                rows, cols = _split_ids(ids, shift)
                rhot = (row_iota == rows).astype(BF16)
                chot = (col_iota == cols).astype(BF16)
                his, los = [], []
                for c in range(comps):
                    p = blk[g, rnd * width + c : rnd * width + c + 1, :]
                    hi = p.astype(BF16)
                    lo = (p - hi.astype(F32)).astype(BF16)
                    his.append(rhot * hi)
                    los.append(rhot * lo)
                lhs = jnp.concatenate(
                    [jnp.concatenate(his, axis=0), jnp.concatenate(los, axis=0)], axis=1
                )
                rhs = jnp.concatenate([chot, chot], axis=1)
                part = lax.dot_general(
                    lhs, rhs, (((1,), (1,)), ((), ())), preferred_element_type=F32
                )
                total = part if total is None else total + part
            out_ref[...] += total
            return carry

        return step

    capacity = recv_ref.shape[1] // width
    for rnd in range(capacity):
        trips = jnp.clip(count_ref[0] - rnd * owners, 0, owners) // 8
        lax.fori_loop(0, trips, make_step(rnd), 0)


def scatter_traction(count, recv, patch_rows, patch_cols, comps):
    shift = patch_cols.bit_length() - 1
    kernel = lambda *refs: _scatter_kernel(*refs, patch_rows=patch_rows, shift=shift, comps=comps)
    out = pl.pallas_call(
        kernel,
        out_shape=jax.ShapeDtypeStruct((comps * patch_rows, patch_cols), F32),
        in_specs=[pl.BlockSpec(memory_space=pltpu.SMEM), pl.BlockSpec(memory_space=pltpu.VMEM)],
        out_specs=pl.BlockSpec(memory_space=pltpu.VMEM),
        name="scatter_traction",
    )(count, recv)
    return out.reshape(comps, patch_rows, patch_cols)


def _gather_kernel(count_ref, recv_ref, field_ref, out_ref, wt_ref, *, patch_rows, shift, width):
    owners, capacity, lanes = out_ref.shape
    patch_cols = 1 << shift
    parts = wt_ref.shape[1] // patch_rows
    field = field_ref[...]
    hi = field.astype(BF16).astype(F32)
    rest = field - hi
    mid = rest.astype(BF16).astype(F32)
    lo = rest - mid
    wt_ref[...] = jnp.concatenate([hi, mid, lo], axis=0).T.astype(BF16)
    row_iota = lax.broadcasted_iota(jnp.int32, (patch_rows, lanes), 0)
    col_iota = lax.broadcasted_iota(jnp.int32, (patch_cols, lanes), 0)
    out_ref[...] = jnp.zeros_like(out_ref)

    def make_step(rnd):
        def step(i, carry):
            base = pl.multiple_of(i * 8, 8)
            blk = recv_ref[pl.ds(base, 8), :, :]
            wt = wt_ref[...]
            outs = []
            for g in range(8):
                ids = blk[g, rnd * width + width - 1 : rnd * width + width, :].astype(jnp.int32)
                rows, cols = _split_ids(ids, shift)
                rhot = (row_iota == rows).astype(BF16)
                rhs = jnp.concatenate([rhot] * parts, axis=0)
                picked = jnp.dot(wt, rhs, preferred_element_type=F32)
                sel = jnp.where(col_iota == cols, picked, 0.0)
                outs.append(jnp.sum(sel, axis=0, keepdims=True))
            out_ref[pl.ds(base, 8), rnd, :] = jnp.concatenate(outs, axis=0)
            return carry

        return step

    for rnd in range(capacity):
        trips = jnp.clip(count_ref[0] - rnd * owners, 0, owners) // 8
        lax.fori_loop(0, trips, make_step(rnd), 0)


def gather_field(count, recv, field, owners, capacity):
    patch_rows, patch_cols = field.shape
    shift = patch_cols.bit_length() - 1
    width = recv.shape[1] // capacity
    kernel = lambda *refs: _gather_kernel(*refs, patch_rows=patch_rows, shift=shift, width=width)
    return pl.pallas_call(
        kernel,
        out_shape=jax.ShapeDtypeStruct((owners, capacity, recv.shape[2]), F32),
        in_specs=[pl.BlockSpec(memory_space=pltpu.SMEM)]
        + [pl.BlockSpec(memory_space=pltpu.VMEM)] * 2,
        out_specs=pl.BlockSpec(memory_space=pltpu.VMEM),
        scratch_shapes=[pltpu.VMEM((patch_cols, 3 * patch_rows), BF16)],
        name="gather_field",
    )(count, recv, field)


def with_halo(x, width):
    ch, rows, cols = x.shape
    n = lax.axis_size("cells")
    m = lax.axis_size("slab")
    slab = lax.axis_index("slab")
    fwd = [(i, (i + 1) % n) for i in range(n)]
    bwd = [((i + 1) % n, i) for i in range(n)]
    left = lax.ppermute(x[:, :, cols - width :], "cells", fwd)
    right = lax.ppermute(x[:, :, :width], "cells", bwd)
    facing = jnp.where(slab == 0, x[:, rows - width :, :], x[:, :width, :])
    swap = [(j, m - 1 - j) for j in range(m)]
    across = lax.ppermute(facing, "slab", swap)
    sides = jnp.concatenate([left, right], axis=2)
    facing_sides = jnp.where(slab == 0, sides[:, rows - width :, :], sides[:, :width, :])
    corners = lax.ppermute(facing_sides, "slab", swap)
    band = jnp.concatenate([left, x, right], axis=2)
    cap = jnp.concatenate([corners[:, :, :width], across, corners[:, :, width:]], axis=2)
    zero = jnp.zeros_like(cap)
    top = jnp.where(slab == 0, zero, cap)
    bottom = jnp.where(slab == 0, cap, zero)
    return jnp.concatenate([top, band, bottom], axis=1)


def on_device(
    block_owner,
    contact_elem,
    grain_offset,
    grain_vel,
    grain_radius,
    disp_cached,
    wall_disp,
    wall_vel,
    wall_stiff,
):
    owners = lax.axis_size("cells")
    blocks = block_owner.shape[0]
    tile_len = contact_elem.shape[0] // blocks
    patch_rows, patch_cols = wall_stiff.shape
    total_cols = patch_cols * owners
    capacity = 2 * (blocks // owners)
    slots = owners * capacity
    width = SUBSTEPS
    elements = contact_elem.reshape(blocks, tile_len)
    radius_tiles = grain_radius.reshape(blocks, tile_len)
    col_index = block_owner[:, None] * patch_cols + elements % patch_cols
    facing_cos, facing_sin = normals(col_index, total_cols)
    push, reach = contact_push(
        grain_offset.reshape(3, blocks, tile_len),
        grain_vel.reshape(3, blocks, tile_len),
        radius_tiles,
        disp_cached.reshape(3, blocks, tile_len),
        facing_cos,
        facing_sin,
    )
    patches = jnp.arange(owners, dtype=jnp.int32)
    member = (block_owner[:, None] == patches[None, :]).astype(jnp.float32)
    tile_ids = jnp.arange(blocks, dtype=jnp.int32)
    before = (tile_ids[None, :] < tile_ids[:, None]).astype(jnp.float32)
    earlier = jnp.dot(before, member, precision=HIGHEST)
    slot = jnp.sum(earlier * member, axis=1).astype(jnp.int32) * owners + block_owner
    placing = (slot[None, :] == jnp.arange(slots, dtype=jnp.int32)[:, None]).astype(jnp.float32)
    sentinel = patch_rows * patch_cols
    payload = jnp.concatenate([push, elements.astype(jnp.float32)[None]], axis=0)
    send = jnp.einsum("sb,cbl->csl", placing, payload, precision=HIGHEST)
    filled = jnp.sum(placing, axis=1) > 0.5
    send = jnp.concatenate(
        [send[:3], jnp.where(filled[:, None], send[3], float(sentinel))[None]], axis=0
    )
    send = jnp.transpose(send.reshape(4, capacity, owners, tile_len), (2, 1, 0, 3))
    recv = lax.all_to_all(
        send.reshape(owners, capacity * 4, tile_len),
        "cells",
        split_axis=0,
        concat_axis=0,
        tiled=True,
    )
    mine = lax.axis_index("cells")
    named = jnp.sum((block_owner == mine).astype(jnp.int32))
    rounds = jnp.clip(named, 1, capacity)
    count = (rounds * owners).reshape(1)

    traction = scatter_traction(count, recv, patch_rows, patch_cols, 3)
    state = jnp.concatenate([wall_disp, wall_vel, wall_stiff[None], traction], axis=0)
    state_ext = with_halo(state, width)
    d_ext, v_ext, stiff_ext = state_ext[:3], state_ext[3:6], state_ext[6]
    traction_ext = state_ext[7:10]

    first_col = lax.axis_index("cells") * patch_cols
    ext_cols = (first_col - width + jnp.arange(patch_cols + 2 * width, dtype=jnp.int32)) % total_cols
    ext_cos, ext_sin = normals(ext_cols, total_cols)
    displace, velocity = (d_ext, v_ext)
    for substep in range(SUBSTEPS):
        padded = jnp.pad(displace, ((0, 0), (1, 1), (0, 0)))
        vertical = padded[:, 2:] + padded[:, :-2]
        padded_c = jnp.pad(displace, ((0, 0), (0, 0), (1, 1)))
        sideways = padded_c[:, :, 2:] + padded_c[:, :, :-2]
        displace, velocity = advance(
            displace, velocity, traction_ext, stiff_ext, vertical, sideways, ext_cos, ext_sin
        )
    wall_next = displace[:, width : width + patch_rows, width : width + patch_cols]
    own_cos = ext_cos[width : width + patch_cols]
    own_sin = ext_sin[width : width + patch_cols]
    radial_field = wall_next[0] * own_cos + wall_next[1] * own_sin
    landed_out = gather_field(count, recv, radial_field, owners, capacity)
    landed_back = lax.all_to_all(
        landed_out, "cells", split_axis=0, concat_axis=0, tiled=True
    ).reshape(slots, tile_len)
    back_slot = block_owner * capacity + jnp.sum(earlier * member, axis=1).astype(jnp.int32)
    taking = (back_slot[None, :] == jnp.arange(slots, dtype=jnp.int32)[:, None]).astype(jnp.float32)
    landed = jnp.einsum("sb,sl->bl", taking, landed_back, precision=HIGHEST)
    contact_gap = radius_tiles + reach - landed
    return (wall_next, contact_gap.reshape(-1))


def solution(mesh):
    return jax.shard_map(
        on_device,
        mesh=mesh,
        in_specs=(
            P(("cells", "slab")),
            P(("cells", "slab")),
            P(None, ("cells", "slab")),
            P(None, ("cells", "slab")),
            P(("cells", "slab")),
            P(None, ("cells", "slab")),
            P(None, "slab", "cells"),
            P(None, "slab", "cells"),
            P("slab", "cells"),
        ),
        out_specs=(P(None, "slab", "cells"), P(("cells", "slab"))),
        check_vma=False,
    )
```
